768 devices in a mesh: band: 6 (over z_lo), pw: 128 (over z_hi, x, y, core).
Axes of the slice: x: 4, y: 8, z: 12 (z_hi: 2, z_lo: 6; z = z_hi * 6 + z_lo), core: 2. Of those that a mesh axis runs over, the one named last changes fastest.
Arguments:
- states: bfloat16 [18, 884736], P('band', 'pw'), may hold values from -12 to 12
- slot_map: int32 [884736], P('pw'), may hold values from 0 to 9215, as said below
- potential: float32 [128, 128, 128], P('pw'), may hold values from -5 to 5
- projectors: bfloat16 [512, 884736], P(None, 'pw'), may hold values from -6 to 6
- species: int32 [64], replicated, may hold values from 0 to 3
- coupling: float32 [4, 8, 8], replicated, may hold values from -2.4 to 2.4
Outputs:
- applied: float32 [18, 884736], P('band', 'pw')
- subspace: float32 [18, 18], P('band')
The draws below stay inside these ranges and needn't reach their ends.
Inputs may be any that keep to these rules, and one draw needn't show every extreme that they name: `slot_map`: within each aligned block of 6912 entries the values are distinct, and each block holds the value 72 * 128 - 1.
All inputs are finite; a program needn't handle non-finite values.
Results may differ from the reference program's by a relative error of at most 0.0019.
Values may be sent and summed in bfloat16 or wider, within the bound.
No kernel may reach another device: no remote copies, remote signals or barrier semaphores. Data moves between devices by JAX's collectives and lax.ppermute only.
A program may use at most 64 MiB of HBM per device.

```python
import math
import jax
import jax.numpy as jnp
from jax import lax

NGRID = 128
NSIDE = 96
NATOM = 64
PA = 8
NSPEC = 4
NBT = 18
NSTK = 9216
STK_DEV = 72
NG = 884736
NG_DEV = 6912
NPROJ = 512
N_PW = 128


def slot_blocks(key):
    slots = STK_DEV * NGRID

    def one_block(block_key):
        perm_key, shift_key = jax.random.split(block_key)
        chosen = jax.random.permutation(perm_key, slots - 1)[:NG_DEV - 1].astype(jnp.int32)
        picked = jnp.concatenate([jnp.full((1,), slots - 1, jnp.int32), chosen])
        return jnp.roll(picked, jax.random.randint(shift_key, (), 0, NG_DEV))
    block_keys = jax.random.split(jax.random.fold_in(key, 17), N_PW)
    return jax.vmap(one_block)(block_keys).astype(jnp.int32)


def draw_slot_map(key, part):
    return slot_blocks(key).reshape(-1).astype(jnp.int32)


def draw_states(key, part):
    noise_key = jax.random.fold_in(jax.random.fold_in(key, 41), 0)
    common_key = jax.random.fold_in(jax.random.fold_in(key, 41), 1)
    mix_key = jax.random.fold_in(jax.random.fold_in(key, 41), 2)
    stick_key = jax.random.fold_in(jax.random.fold_in(key, 41), 4)
    phase_key = jax.random.fold_in(jax.random.fold_in(key, 41), 5)
    layout = slot_blocks(key)
    first = (jnp.arange(N_PW).astype(jnp.int32) * STK_DEV)[:, None]
    sticks = (first + layout % STK_DEV).reshape(-1).astype(jnp.int32)
    planes = (layout // STK_DEV).reshape(-1).astype(jnp.float32)
    phases = jax.random.uniform(phase_key, (NBT, 1), jnp.float32, -math.pi, math.pi)
    waves = jnp.cos(planes[None, :] * (2.0 * math.pi / NGRID) + phases)
    noise = jnp.clip(jax.random.normal(noise_key, (NBT, NG), jnp.float32), -4.0, 4.0)
    common = jnp.clip(jax.random.normal(common_key, (NG,), jnp.float32), -4.0, 4.0)
    stick_amp = jnp.clip(jax.random.normal(stick_key, (NBT, NSTK), jnp.float32), -3.0, 3.0)
    envelope = stick_amp[:, sticks]
    mixing = jax.random.uniform(mix_key, (NBT, 1), jnp.float32, 0.5, 1.0)
    rough = 0.5 * (noise + mixing * common[None, :])
    return (rough + 0.8 * envelope * waves).astype(jnp.bfloat16)


def draw_potential(key, part):
    rough_key, sign_key, amp_key = jax.random.split(jax.random.fold_in(key, 29), 3)
    planes = jnp.arange(NGRID).astype(jnp.float32)
    wave = jnp.cos(planes * (2.0 * math.pi / NGRID))
    sign = (jax.random.randint(sign_key, (), 0, 2) * 2 - 1).astype(jnp.float32)
    rough = jnp.clip(jax.random.normal(rough_key, (NGRID, NGRID, NGRID), jnp.float32), -3.0, 3.0)
    amplitude = jax.random.uniform(amp_key, (), jnp.float32, 1.5, 2.0)
    smooth = amplitude * sign * wave
    return (smooth[:, None, None] + rough).astype(jnp.float32)


def place_ends(drawn, rng, least, high):
    extent = drawn.shape
    spot = [jax.random.randint(jax.random.fold_in(rng, axis), (), 0, extent[axis]) for axis in range(len(extent))]
    drawn = drawn.at[tuple(spot)].set(least)
    longest = extent.index(max(extent))
    spot[longest] = (spot[longest] + 1) % extent[longest]
    return drawn.at[tuple(spot)].set(high)


def shard_levels(own_key, shape, shards, smallest, top_value):
    gain = 1.0
    for position, shards_of in shards:
        steps = jax.random.uniform(jax.random.fold_in(jax.random.fold_in(own_key, 6), position), (shards_of,), jnp.float32, smallest / len(shards), top_value / len(shards))
        gain = gain * jnp.repeat(jnp.exp(steps), shape[position] // shards_of).reshape((-1,) + (1,) * (len(shape) - 1 - position))
    return gain


def normal_values(key, dims, spread, most, pieces=(), kind=jnp.bfloat16):
    drawn = spread * jax.random.normal(key, dims, jnp.float32)
    if pieces:
        drawn = drawn * shard_levels(key, dims, pieces, -0.22, 0.18)
    return jnp.clip(drawn, -most, most).astype(kind)


def setup_inputs(seed: int = 0) -> dict:
    keys = jax.random.split(jax.random.key(seed), 7)
    return {
        "states": draw_states(jax.random.fold_in(keys[6], 71), 0),
        "slot_map": draw_slot_map(jax.random.fold_in(keys[6], 71), 0),
        "potential": draw_potential(jax.random.fold_in(keys[6], 71), 0),
        "projectors": normal_values(keys[3], (NPROJ, NG), 1.0, 6.0, ((1, 128),)),
        "species": place_ends(jax.random.randint(keys[4], (NATOM,), 0, NSPEC), jax.random.fold_in(keys[4], 1), 0, NSPEC - 1).astype(jnp.int32),
        "coupling": normal_values(keys[5], (NSPEC, PA, PA), 0.4, 2.4, (), jnp.float32),
    }


def cas_table(frequency, length):
    columns = jnp.arange(length).astype(jnp.int32)
    phases = frequency.astype(jnp.int32)[:, None] * columns[None, :] % length
    angles = phases.astype(jnp.float32) * (2.0 * math.pi / length)
    return (jnp.cos(angles) + jnp.sin(angles)) / math.sqrt(length)

def side_frequency(indices):
    halves = (indices + 1) // 2
    return jnp.where(indices % 2 == 1, halves, -halves)

def kinetic(slot_map, first_stick, stick_count, length, side):
    sticks = first_stick + slot_map % stick_count
    plane_index = slot_map // stick_count
    along_z = jnp.where(plane_index < length // 2, plane_index, plane_index - length)
    along_x = side_frequency(sticks // side)
    along_y = side_frequency(sticks % side)
    squared = along_x * along_x + along_y * along_y + along_z * along_z
    return squared.astype(jnp.float32) * (1.0 / (0.5 * side * side + 0.25 * length * length))

def reference(states, slot_map, potential, projectors, species, coupling):
    highest = lax.Precision.HIGHEST
    total, count = states.shape
    length = NGRID
    side = NSIDE
    stick_count = STK_DEV
    blocks = (jnp.arange(count).astype(jnp.int32) // NG_DEV).astype(jnp.int32)
    first = (blocks * stick_count).astype(jnp.int32)
    sticks = (first + slot_map % stick_count).astype(jnp.int32)
    plane_index = (slot_map // stick_count).astype(jnp.int32)
    wide = states.astype(jnp.float32)
    dense = jnp.zeros((total, length, NSTK), jnp.float32).at[:, plane_index, sticks].set(wide)
    z_table = cas_table(jnp.arange(length).astype(jnp.int32), length)
    side_table = cas_table(side_frequency(jnp.arange(side).astype(jnp.int32)), length)
    columns = jnp.einsum('bks,kz->bzs', dense, z_table, precision=highest)
    grid = columns.reshape(total, length, side, side)
    half = jnp.einsum('bzjk,jx->bzxk', grid, side_table, precision=highest)
    real_space = jnp.einsum('bzxk,ky->bzxy', half, side_table, precision=highest)
    weighted = real_space * potential[None]
    back_half = jnp.einsum('bzxy,ky->bzxk', weighted, side_table, precision=highest)
    back_grid = jnp.einsum('bzxk,jx->bzjk', back_half, side_table, precision=highest)
    returned = back_grid.reshape(total, length, NSTK)
    spectral = jnp.einsum('bzs,kz->bks', returned, z_table, precision=highest)
    local_term = spectral[:, plane_index, sticks]
    energies = kinetic(slot_map, first, stick_count, length, side)
    partial_value = lax.dot_general(projectors, states, (((1,), (1,)), ((), ())), preferred_element_type=jnp.float32)
    correlations = partial_value / math.sqrt(NG)
    atoms = species.shape[0]
    per_atom = coupling.shape[1]
    kinds = coupling.shape[0]
    symmetric = 0.5 * (coupling + jnp.swapaxes(coupling, 1, 2))
    onehot = (species[:, None] == jnp.arange(kinds).astype(jnp.int32)[None, :]).astype(jnp.float32)
    chosen = jnp.einsum('as,smn->amn', onehot, symmetric, precision=highest)
    weights = jnp.einsum('amn,anb->amb', chosen, correlations.reshape(atoms, per_atom, total), precision=highest)
    weights = weights.reshape(atoms * per_atom, total).astype(jnp.bfloat16)
    nonlocal_term = lax.dot_general(weights, projectors, (((0,), (0,)), ((), ())), preferred_element_type=jnp.float32) / math.sqrt(atoms * per_atom)
    applied = energies[None, :] * wide + local_term + nonlocal_term
    subspace = lax.dot_general(wide, applied, (((1,), (1,)), ((), ())), precision=highest, preferred_element_type=jnp.float32) / float(NG)
    return (applied, subspace)
```

```python
import functools
import math

import jax
import jax.numpy as jnp
from jax import lax
from jax.sharding import Mesh
from jax.sharding import PartitionSpec as P

NSIDE = 96
NG = 884736
PW = ("pw_0", "pw_1", "pw_2", "pw_3")


def cut_along(x, dim, length):
    shape = x.shape
    pieces = x.reshape(*shape[:dim], length, shape[dim] // length, *shape[dim + 1 :])
    return jnp.moveaxis(pieces, dim, 0)


def joined_along(pieces, dim):
    pieces = jnp.moveaxis(pieces, 0, dim)
    shape = pieces.shape
    return pieces.reshape(*shape[:dim], shape[dim] * shape[dim + 1], *shape[dim + 2 :])


def moved_by_axis(pieces, axes, order):
    inside = pieces.shape[1:]
    whole = pieces.reshape(*(lax.axis_size(a) for a in axes), *inside)
    for k in order:
        whole = lax.all_to_all(whole, axes[k], k, k, tiled=True)
    return whole.reshape(-1, *inside)


def exchange_by_chip(x, groups, order, split_dim, concat_dim):
    length = lax.axis_size(groups[0]) * lax.axis_size(groups[1])
    pieces = cut_along(x, split_dim, length)
    return joined_along(moved_by_axis(pieces, groups, order), concat_dim)


def one_axis_at_a_time(x, axes):
    return functools.reduce(lax.psum, axes, x)


def from_everyone(x, axis):
    length = lax.axis_size(axis)
    return lax.all_to_all(jnp.broadcast_to(x[None], (length, *x.shape)), axis, 0, 0, tiled=True)


def collect(x, axis, dim):
    return joined_along(from_everyone(x, axis), dim)


def cas_table(frequency, length):
    columns = jnp.arange(length)
    phases = frequency[:, None] * columns[None, :] % length
    angles = phases.astype(jnp.float32) * (2.0 * math.pi / length)
    return (jnp.cos(angles) + jnp.sin(angles)) / math.sqrt(length)


def side_frequency(indices):
    halves = (indices + 1) // 2
    return jnp.where(indices % 2 == 1, halves, -halves)


def kinetic(slot_map, first_stick, stick_count, length, side):
    sticks = first_stick + slot_map % stick_count
    plane_index = slot_map // stick_count
    along_z = jnp.where(plane_index < length // 2, plane_index, plane_index - length)
    along_x = side_frequency(sticks // side)
    along_y = side_frequency(sticks % side)
    squared = along_x * along_x + along_y * along_y + along_z * along_z
    return squared.astype(jnp.float32) * (1.0 / (0.5 * side * side + 0.25 * length * length))


def local(states, slot_map, potential, projectors, species, coupling):
    highest = lax.Precision.HIGHEST
    bands = states.shape[0]
    planes = potential.shape[0]
    length = potential.shape[1]
    side = NSIDE
    stick_count = side * side // lax.axis_size(PW)
    owner = lax.axis_index(PW)
    wide = states.astype(jnp.float32)
    dense = jnp.zeros((bands, length * stick_count), jnp.float32).at[:, slot_map].set(wide)
    dense = dense.reshape(bands, length, stick_count)
    z_table = cas_table(jnp.arange(length), length)
    side_table = cas_table(side_frequency(jnp.arange(side)), length)
    columns = jnp.einsum("bks,kz->bzs", dense, z_table, precision=highest)
    piece = lax.all_to_all(columns, PW, split_axis=1, concat_axis=2, tiled=True)
    count = piece.shape[0]
    grid = piece.reshape(count, planes, side, side)
    half = jnp.einsum("bzjk,jx->bzxk", grid, side_table, precision=highest)
    real_space = jnp.einsum("bzxk,ky->bzxy", half, side_table, precision=highest)
    weighted = real_space * potential[None]
    back_half = jnp.einsum("bzxy,ky->bzxk", weighted, side_table, precision=highest)
    back_grid = jnp.einsum("bzxk,jx->bzjk", back_half, side_table, precision=highest)
    returned = lax.all_to_all(
        back_grid.reshape(count, planes, side * side), PW, split_axis=2, concat_axis=1, tiled=True
    )
    spectral = jnp.einsum("bzs,kz->bks", returned, z_table, precision=highest)
    local_term = spectral.reshape(bands, length * stick_count)[:, slot_map]
    energies = kinetic(slot_map, owner * stick_count, stick_count, length, side)
    partial_value = lax.dot_general(
        projectors, states, (((1,), (1,)), ((), ())), preferred_element_type=jnp.float32
    )
    correlations = lax.psum(partial_value, PW) / math.sqrt(NG)
    atoms = species.shape[0]
    per_atom = coupling.shape[1]
    kinds = coupling.shape[0]
    symmetric = 0.5 * (coupling + jnp.swapaxes(coupling, 1, 2))
    onehot = (species[:, None] == jnp.arange(kinds)[None, :]).astype(jnp.float32)
    chosen = jnp.einsum("as,smn->amn", onehot, symmetric, precision=highest)
    weights = jnp.einsum(
        "amn,anb->amb", chosen, correlations.reshape(atoms, per_atom, bands), precision=highest
    )
    weights = weights.reshape(atoms * per_atom, bands).astype(jnp.bfloat16)
    nonlocal_term = lax.dot_general(
        weights, projectors, (((0,), (0,)), ((), ())), preferred_element_type=jnp.float32
    ) / math.sqrt(atoms * per_atom)
    applied = energies[None, :] * wide + local_term + nonlocal_term
    group = lax.axis_index("band")
    every_state = lax.all_gather(states, "band", axis=0, tiled=True).astype(jnp.float32)
    block = lax.dot_general(
        every_state,
        applied,
        (((1,), (1,)), ((), ())),
        precision=highest,
        preferred_element_type=jnp.float32,
    )
    total = every_state.shape[0]
    placed = lax.dynamic_update_slice(
        jnp.zeros((total, total), jnp.float32), block, (0, group * bands)
    )
    whole = lax.psum(placed, ("band",) + PW) / float(NG)
    subspace = lax.dynamic_slice(whole, (group * bands, 0), (bands, total))
    return (applied, subspace)


def solution(mesh):
    split = Mesh(
        mesh.devices.reshape(mesh.shape["band"], 2, 4, 8, 2),
        ("band", "pw_0", "pw_1", "pw_2", "pw_3"),
    )
    return jax.shard_map(
        local,
        mesh=split,
        in_specs=(P("band", PW), P(PW), P(PW, None, None), P(None, PW), P(), P()),
        out_specs=(P("band", PW), P("band", None)),
        check_vma=False,
    )
```

```python
import math

import jax
import jax.numpy as jnp
from jax import lax
from jax.sharding import Mesh
from jax.sharding import PartitionSpec as P

NSIDE = 96
NG = 884736
PW = ("pw_0", "pw_1", "pw_2", "pw_3")


def one_axis_at_a_time(x, axes):
    for a in axes:
        x = lax.psum(x, a)
    return x


def cas_table(frequency, length):
    columns = jnp.arange(length)
    phases = frequency[:, None] * columns[None, :] % length
    angles = phases.astype(jnp.float32) * (2.0 * math.pi / length)
    return (jnp.cos(angles) + jnp.sin(angles)) / math.sqrt(length)


def side_frequency(indices):
    halves = (indices + 1) // 2
    return jnp.where(indices % 2 == 1, halves, -halves)


def kinetic(slot_map, first_stick, stick_count, length, side):
    sticks = first_stick + slot_map % stick_count
    plane_index = slot_map // stick_count
    along_z = jnp.where(plane_index < length // 2, plane_index, plane_index - length)
    along_x = side_frequency(sticks // side)
    along_y = side_frequency(sticks % side)
    squared = along_x * along_x + along_y * along_y + along_z * along_z
    return squared.astype(jnp.float32) * (1.0 / (0.5 * side * side + 0.25 * length * length))


def gathered_bands(states, axis):
    n = lax.axis_size(axis)
    blocks = [states]
    for k in range(1, n):
        blocks.append(lax.ppermute(states, axis, [(i, (i + k) % n) for i in range(n)]))
    return jnp.concatenate(blocks, axis=0)


def local(states, slot_map, potential, projectors, species, coupling):
    highest = lax.Precision.HIGHEST
    bands = states.shape[0]
    planes = potential.shape[0]
    length = potential.shape[1]
    side = NSIDE
    npw = lax.axis_size(PW)
    stick_count = side * side // npw
    owner = lax.axis_index(PW)
    group = lax.axis_index("band")
    ngroup = lax.axis_size("band")
    every = gathered_bands(states, "band")
    total = every.shape[0]
    wide = states.astype(jnp.float32)
    dense = jnp.zeros((bands, length * stick_count), jnp.float32).at[:, slot_map].set(wide)
    dense = dense.reshape(bands, length, stick_count)
    z_table = cas_table(jnp.arange(length), length)
    side_table = cas_table(side_frequency(jnp.arange(side)), length)
    columns = jnp.einsum("bks,kz->zbs", dense, z_table, precision=highest)
    sent = columns.reshape(npw, planes * bands * stick_count)
    piece = lax.all_to_all(sent, PW, 0, 0, tiled=True)
    piece = piece.reshape(npw, planes, bands, stick_count)
    grid = jnp.transpose(piece, (2, 1, 0, 3)).reshape(bands, planes, side, side)
    half = jnp.einsum("bzjk,jx->bzxk", grid, side_table, precision=highest)
    real_space = jnp.einsum("bzxk,ky->bzxy", half, side_table, precision=highest)
    weighted = real_space * potential[None]
    back_half = jnp.einsum("bzxy,ky->bzxk", weighted, side_table, precision=highest)
    back_grid = jnp.einsum("bzxk,jx->bzjk", back_half, side_table, precision=highest)
    back = back_grid.reshape(bands, planes, npw, stick_count)
    back = jnp.transpose(back, (2, 1, 0, 3)).reshape(npw, planes * bands * stick_count)
    returned = lax.all_to_all(back, PW, 0, 0, tiled=True)
    returned = returned.reshape(npw * planes, bands, stick_count)
    spectral = jnp.einsum("zbs,kz->bks", returned, z_table, precision=highest)
    local_term = spectral.reshape(bands, length * stick_count)[:, slot_map]
    energies = kinetic(slot_map, owner * stick_count, stick_count, length, side)
    diagonal = energies[None, :] * wide + local_term
    partial_corr = lax.dot_general(
        projectors, every, (((1,), (1,)), ((), ())), preferred_element_type=jnp.float32
    )
    partial_gram = lax.dot_general(
        diagonal,
        every.astype(jnp.float32),
        (((1,), (1,)), ((), ())),
        precision=highest,
        preferred_element_type=jnp.float32,
    )
    nproj = partial_corr.shape[0]
    packed = jnp.concatenate([partial_corr.reshape(-1), partial_gram.reshape(-1)])
    reduced = one_axis_at_a_time(packed, PW)
    correlations = reduced[: nproj * total].reshape(nproj, total) / math.sqrt(NG)
    gram = reduced[nproj * total :].reshape(bands, total)
    atoms = species.shape[0]
    per_atom = coupling.shape[1]
    kinds = coupling.shape[0]
    symmetric = 0.5 * (coupling + jnp.swapaxes(coupling, 1, 2))
    onehot = (species[:, None] == jnp.arange(kinds)[None, :]).astype(jnp.float32)
    chosen = jnp.einsum("as,smn->amn", onehot, symmetric, precision=highest)
    weights = jnp.einsum(
        "amn,anb->amb", chosen, correlations.reshape(atoms, per_atom, total), precision=highest
    )
    weights = weights.reshape(atoms * per_atom, total).astype(jnp.bfloat16)
    nonlocal_term = lax.dot_general(
        weights[:, :bands], projectors, (((0,), (0,)), ((), ())), preferred_element_type=jnp.float32
    ) / math.sqrt(atoms * per_atom)
    applied = diagonal + nonlocal_term
    cross = lax.dot_general(
        correlations[:, :bands],
        weights.astype(jnp.float32),
        (((0,), (0,)), ((), ())),
        precision=highest,
        preferred_element_type=jnp.float32,
    ) / (math.sqrt(atoms * per_atom) * math.sqrt(NG))
    rotated = (gram / float(NG) + cross).reshape(bands, ngroup, bands)
    order = (group - jnp.arange(ngroup)) % ngroup
    subspace = jnp.take(rotated, order, axis=1).reshape(bands, total)
    return (applied, subspace)


def solution(mesh):
    split = Mesh(
        mesh.devices.reshape(mesh.shape["band"], 2, 4, 8, 2),
        ("band", "pw_0", "pw_1", "pw_2", "pw_3"),
    )
    return jax.shard_map(
        local,
        mesh=split,
        in_specs=(P("band", PW), P(PW), P(PW, None, None), P(None, PW), P(), P()),
        out_specs=(P("band", PW), P("band", None)),
        check_vma=False,
    )
```

```python
import math

import jax
import jax.numpy as jnp
from jax import lax
from jax.sharding import Mesh
from jax.sharding import PartitionSpec as P

NSIDE = 96
NG = 884736
PW = ("pw_0", "pw_1", "pw_2", "pw_3")


def one_axis_at_a_time(x, axes):
    for a in axes:
        x = lax.psum(x, a)
    return x


def butterfly(x, axes):
    for a in axes:
        n = lax.axis_size(a)
        d = 1
        while d < n:
            x = x + lax.ppermute(x, a, [(i, i ^ d) for i in range(n)])
            d *= 2
    return x


def cas_table(frequency, length):
    columns = jnp.arange(length)
    phases = frequency[:, None] * columns[None, :] % length
    angles = phases.astype(jnp.float32) * (2.0 * math.pi / length)
    return (jnp.cos(angles) + jnp.sin(angles)) / math.sqrt(length)


def side_frequency(indices):
    halves = (indices + 1) // 2
    return jnp.where(indices % 2 == 1, halves, -halves)


def kinetic(slot_map, first_stick, stick_count, length, side):
    sticks = first_stick + slot_map % stick_count
    plane_index = slot_map // stick_count
    along_z = jnp.where(plane_index < length // 2, plane_index, plane_index - length)
    along_x = side_frequency(sticks // side)
    along_y = side_frequency(sticks % side)
    squared = along_x * along_x + along_y * along_y + along_z * along_z
    return squared.astype(jnp.float32) * (1.0 / (0.5 * side * side + 0.25 * length * length))


def gathered_bands(states, axis):
    n = lax.axis_size(axis)
    blocks = [states]
    for k in range(1, n):
        blocks.append(lax.ppermute(states, axis, [(i, (i + k) % n) for i in range(n)]))
    return jnp.concatenate(blocks, axis=0)


def local(states, slot_map, potential, projectors, species, coupling):
    highest = lax.Precision.HIGHEST
    bands = states.shape[0]
    planes = potential.shape[0]
    length = potential.shape[1]
    side = NSIDE
    npw = lax.axis_size(PW)
    stick_count = side * side // npw
    owner = lax.axis_index(PW)
    group = lax.axis_index("band")
    ngroup = lax.axis_size("band")
    every = gathered_bands(states, "band")
    total = every.shape[0]
    wide = states.astype(jnp.float32)
    plane_of = slot_map // stick_count
    stick_of = slot_map % stick_count
    on_stick = (stick_of[:, None] == jnp.arange(stick_count)[None, :]).astype(jnp.bfloat16)
    on_plane = jnp.arange(length)[:, None] == plane_of[None, :]
    spread = jnp.where(on_plane[None], states[:, None, :], jnp.zeros((), states.dtype))
    dense = jnp.dot(
        spread.reshape(bands * length, -1), on_stick, preferred_element_type=jnp.float32
    ).reshape(bands, length, stick_count)
    z_table = cas_table(jnp.arange(length), length)
    side_table = cas_table(side_frequency(jnp.arange(side)), length)
    columns = jnp.einsum("bks,kz->zbs", dense, z_table, precision=highest)
    sent = columns.reshape(npw, planes * bands * stick_count)
    piece = lax.all_to_all(sent, PW, 0, 0, tiled=True)
    piece = piece.reshape(npw, planes, bands, stick_count)
    grid = jnp.transpose(piece, (2, 1, 0, 3)).reshape(bands, planes, side, side)
    half = jnp.einsum("bzjk,jx->bzxk", grid, side_table, precision=highest)
    real_space = jnp.einsum("bzxk,ky->bzxy", half, side_table, precision=highest)
    weighted = real_space * potential[None]
    back_half = jnp.einsum("bzxy,ky->bzxk", weighted, side_table, precision=highest)
    back_grid = jnp.einsum("bzxk,jx->bzjk", back_half, side_table, precision=highest)
    back = back_grid.reshape(bands, planes, npw, stick_count)
    back = jnp.transpose(back, (2, 1, 0, 3)).reshape(npw, planes * bands * stick_count)
    returned = lax.all_to_all(back, PW, 0, 0, tiled=True)
    returned = returned.reshape(npw * planes, bands, stick_count)
    spectral = jnp.einsum("zbs,kz->bks", returned, z_table, precision=highest)
    picked = jnp.dot(
        spectral.reshape(bands * length, stick_count),
        on_stick.T.astype(jnp.float32),
        precision=highest,
        preferred_element_type=jnp.float32,
    ).reshape(bands, length, -1)
    local_term = jnp.sum(jnp.where(on_plane[None], picked, 0.0), axis=1)
    energies = kinetic(slot_map, owner * stick_count, stick_count, length, side)
    diagonal = energies[None, :] * wide + local_term
    partial_corr = lax.dot_general(
        projectors, every, (((1,), (1,)), ((), ())), preferred_element_type=jnp.float32
    )
    partial_gram = lax.dot_general(
        diagonal,
        every.astype(jnp.float32),
        (((1,), (1,)), ((), ())),
        precision=highest,
        preferred_element_type=jnp.float32,
    )
    nproj = partial_corr.shape[0]
    packed = jnp.concatenate([partial_corr.reshape(-1), partial_gram.reshape(-1)])
    reduced = butterfly(packed, PW)
    correlations = reduced[: nproj * total].reshape(nproj, total) / math.sqrt(NG)
    gram = reduced[nproj * total :].reshape(bands, total)
    atoms = species.shape[0]
    per_atom = coupling.shape[1]
    kinds = coupling.shape[0]
    symmetric = 0.5 * (coupling + jnp.swapaxes(coupling, 1, 2))
    onehot = (species[:, None] == jnp.arange(kinds)[None, :]).astype(jnp.float32)
    chosen = jnp.einsum("as,smn->amn", onehot, symmetric, precision=highest)
    weights = jnp.einsum(
        "amn,anb->amb", chosen, correlations.reshape(atoms, per_atom, total), precision=highest
    )
    weights = weights.reshape(atoms * per_atom, total).astype(jnp.bfloat16)
    nonlocal_term = lax.dot_general(
        weights[:, :bands], projectors, (((0,), (0,)), ((), ())), preferred_element_type=jnp.float32
    ) / math.sqrt(atoms * per_atom)
    applied = diagonal + nonlocal_term
    cross = lax.dot_general(
        correlations[:, :bands],
        weights.astype(jnp.float32),
        (((0,), (0,)), ((), ())),
        precision=highest,
        preferred_element_type=jnp.float32,
    ) / (math.sqrt(atoms * per_atom) * math.sqrt(NG))
    rotated = (gram / float(NG) + cross).reshape(bands, ngroup, bands)
    order = (group - jnp.arange(ngroup)) % ngroup
    subspace = jnp.take(rotated, order, axis=1).reshape(bands, total)
    return (applied, subspace)


def solution(mesh):
    split = Mesh(
        mesh.devices.reshape(mesh.shape["band"], 2, 4, 8, 2),
        ("band", "pw_0", "pw_1", "pw_2", "pw_3"),
    )
    return jax.shard_map(
        local,
        mesh=split,
        in_specs=(P("band", PW), P(PW), P(PW, None, None), P(None, PW), P(), P()),
        out_specs=(P("band", PW), P("band", None)),
        check_vma=False,
    )
```

```python
import math

import jax
import jax.numpy as jnp
from jax import lax
from jax.sharding import Mesh
from jax.sharding import PartitionSpec as P

NSIDE = 96
NG = 884736
PW = ("pw_0", "pw_1", "pw_2", "pw_3")


def one_axis_at_a_time(x, axes):
    for a in axes:
        x = lax.psum(x, a)
    return x


def butterfly(x, axes):
    for a in axes:
        n = lax.axis_size(a)
        d = 1
        while d < n:
            x = x + lax.ppermute(x, a, [(i, i ^ d) for i in range(n)])
            d *= 2
    return x


def cas_table(frequency, length):
    columns = jnp.arange(length)
    phases = frequency[:, None] * columns[None, :] % length
    angles = phases.astype(jnp.float32) * (2.0 * math.pi / length)
    return (jnp.cos(angles) + jnp.sin(angles)) / math.sqrt(length)


def side_frequency(indices):
    halves = (indices + 1) // 2
    return jnp.where(indices % 2 == 1, halves, -halves)


def kinetic(slot_map, first_stick, stick_count, length, side):
    sticks = first_stick + slot_map % stick_count
    plane_index = slot_map // stick_count
    along_z = jnp.where(plane_index < length // 2, plane_index, plane_index - length)
    along_x = side_frequency(sticks // side)
    along_y = side_frequency(sticks % side)
    squared = along_x * along_x + along_y * along_y + along_z * along_z
    return squared.astype(jnp.float32) * (1.0 / (0.5 * side * side + 0.25 * length * length))


def gathered_bands(states, axis):
    n = lax.axis_size(axis)
    blocks = [states]
    for k in range(1, n):
        blocks.append(lax.ppermute(states, axis, [(i, (i + k) % n) for i in range(n)]))
    return jnp.concatenate(blocks, axis=0)


def local(states, slot_map, potential, projectors, species, coupling):
    highest = lax.Precision.HIGHEST
    bands = states.shape[0]
    planes = potential.shape[0]
    length = potential.shape[1]
    side = NSIDE
    npw = lax.axis_size(PW)
    stick_count = side * side // npw
    owner = lax.axis_index(PW)
    group = lax.axis_index("band")
    ngroup = lax.axis_size("band")
    every = gathered_bands(states, "band")
    total = every.shape[0]
    count = states.shape[1]
    wide = states.astype(jnp.float32)
    plane_of = slot_map // stick_count
    stick_of = slot_map % stick_count
    on_stick = stick_of[:, None] == jnp.arange(stick_count)[None, :]
    on_plane = jnp.arange(length)[:, None] == plane_of[None, :]
    spread = jnp.where(on_stick[:, None, :], every.T[:, :, None], jnp.zeros((), every.dtype))
    dense = jnp.dot(
        on_plane.astype(jnp.bfloat16),
        spread.reshape(count, total * stick_count),
        preferred_element_type=jnp.float32,
    )
    z_table = cas_table(jnp.arange(length), length)
    side_table = cas_table(side_frequency(jnp.arange(side)), length)
    columns = jnp.dot(z_table.T, dense, precision=highest, preferred_element_type=jnp.float32)
    energies = kinetic(slot_map, owner * stick_count, stick_count, length, side)
    partial_corr = lax.dot_general(
        projectors, every, (((1,), (1,)), ((), ())), preferred_element_type=jnp.float32
    )
    partial_kin = lax.dot_general(
        energies[None, :] * wide,
        every.astype(jnp.float32),
        (((1,), (1,)), ((), ())),
        precision=highest,
        preferred_element_type=jnp.float32,
    )
    nproj = partial_corr.shape[0]
    packed = jnp.concatenate([partial_corr.reshape(-1), partial_kin.reshape(-1)])
    width = -(-packed.shape[0] // npw)
    packed = jnp.pad(packed, (0, width * npw - packed.shape[0])).reshape(npw, width)
    sent = jnp.concatenate([columns.reshape(npw, planes * total * stick_count), packed], axis=1)
    got = lax.all_to_all(sent, PW, 0, 0, tiled=True)
    piece = got[:, : planes * total * stick_count].reshape(npw, total, stick_count)
    owned = jnp.sum(got[:, planes * total * stick_count :], axis=0)
    grid = jnp.transpose(piece[:, :bands, :], (1, 0, 2)).reshape(bands, planes, side, side)
    half = jnp.einsum("bzjk,jx->bzxk", grid, side_table, precision=highest)
    real_space = jnp.einsum("bzxk,ky->bzxy", half, side_table, precision=highest)
    weighted = real_space * potential[None]
    back_half = jnp.einsum("bzxy,ky->bzxk", weighted, side_table, precision=highest)
    back_grid = jnp.einsum("bzxk,jx->bzjk", back_half, side_table, precision=highest)
    back_own = back_grid.reshape(bands, side * side)
    plane_gram = lax.dot_general(
        back_own,
        jnp.transpose(piece, (1, 0, 2)).reshape(total, side * side),
        (((1,), (1,)), ((), ())),
        precision=highest,
        preferred_element_type=jnp.float32,
    )
    back = jnp.transpose(back_own.reshape(bands, npw, stick_count), (1, 0, 2))
    ret_sent = jnp.concatenate(
        [
            back.reshape(npw, bands * stick_count),
            jnp.broadcast_to(plane_gram.reshape(1, -1), (npw, bands * total)),
            jnp.broadcast_to(owned[None, :], (npw, width)),
        ],
        axis=1,
    )
    ret = lax.all_to_all(ret_sent, PW, 0, 0, tiled=True)
    returned = ret[:, : bands * stick_count].reshape(npw * planes, bands, stick_count)
    gram_local = jnp.sum(
        ret[:, bands * stick_count : bands * stick_count + bands * total], axis=0
    ).reshape(bands, total)
    reduced = ret[:, bands * stick_count + bands * total :].reshape(-1)
    correlations = reduced[: nproj * total].reshape(nproj, total) / math.sqrt(NG)
    gram_kin = reduced[nproj * total : nproj * total + bands * total].reshape(bands, total)
    spectral = jnp.einsum("zbs,kz->bks", returned, z_table, precision=highest)
    picked = jnp.dot(
        spectral.reshape(bands * length, stick_count),
        on_stick.T.astype(jnp.float32),
        precision=highest,
        preferred_element_type=jnp.float32,
    ).reshape(bands, length, -1)
    local_term = jnp.sum(jnp.where(on_plane[None], picked, 0.0), axis=1)
    atoms = species.shape[0]
    per_atom = coupling.shape[1]
    kinds = coupling.shape[0]
    symmetric = 0.5 * (coupling + jnp.swapaxes(coupling, 1, 2))
    onehot = (species[:, None] == jnp.arange(kinds)[None, :]).astype(jnp.float32)
    chosen = jnp.einsum("as,smn->amn", onehot, symmetric, precision=highest)
    weights = jnp.einsum(
        "amn,anb->amb", chosen, correlations.reshape(atoms, per_atom, total), precision=highest
    )
    weights = weights.reshape(atoms * per_atom, total).astype(jnp.bfloat16)
    nonlocal_term = lax.dot_general(
        weights[:, :bands], projectors, (((0,), (0,)), ((), ())), preferred_element_type=jnp.float32
    ) / math.sqrt(atoms * per_atom)
    applied = energies[None, :] * wide + local_term + nonlocal_term
    cross = lax.dot_general(
        correlations[:, :bands],
        weights.astype(jnp.float32),
        (((0,), (0,)), ((), ())),
        precision=highest,
        preferred_element_type=jnp.float32,
    ) / (math.sqrt(atoms * per_atom) * math.sqrt(NG))
    rotated = ((gram_kin + gram_local) / float(NG) + cross).reshape(bands, ngroup, bands)
    order = (group - jnp.arange(ngroup)) % ngroup
    subspace = jnp.take(rotated, order, axis=1).reshape(bands, total)
    return (applied, subspace)


def solution(mesh):
    split = Mesh(
        mesh.devices.reshape(mesh.shape["band"], 2, 4, 8, 2),
        ("band", "pw_0", "pw_1", "pw_2", "pw_3"),
    )
    return jax.shard_map(
        local,
        mesh=split,
        in_specs=(P("band", PW), P(PW), P(PW, None, None), P(None, PW), P(), P()),
        out_specs=(P("band", PW), P("band", None)),
        check_vma=False,
    )
```

```python
import math

import jax
import jax.numpy as jnp
from jax import lax
from jax.sharding import Mesh
from jax.sharding import PartitionSpec as P

NSIDE = 96
NG = 884736
PW = ("pw_0", "pw_1", "pw_2", "pw_3")


def one_axis_at_a_time(x, axes):
    for a in axes:
        x = lax.psum(x, a)
    return x


def butterfly(x, axes):
    for a in axes:
        n = lax.axis_size(a)
        d = 1
        while d < n:
            x = x + lax.ppermute(x, a, [(i, i ^ d) for i in range(n)])
            d *= 2
    return x


def cas_table(frequency, length):
    columns = jnp.arange(length)
    phases = frequency[:, None] * columns[None, :] % length
    angles = phases.astype(jnp.float32) * (2.0 * math.pi / length)
    return (jnp.cos(angles) + jnp.sin(angles)) / math.sqrt(length)


def side_frequency(indices):
    halves = (indices + 1) // 2
    return jnp.where(indices % 2 == 1, halves, -halves)


def kinetic(slot_map, first_stick, stick_count, length, side):
    sticks = first_stick + slot_map % stick_count
    plane_index = slot_map // stick_count
    along_z = jnp.where(plane_index < length // 2, plane_index, plane_index - length)
    along_x = side_frequency(sticks // side)
    along_y = side_frequency(sticks % side)
    squared = along_x * along_x + along_y * along_y + along_z * along_z
    return squared.astype(jnp.float32) * (1.0 / (0.5 * side * side + 0.25 * length * length))


def gathered_bands(states, axis):
    n = lax.axis_size(axis)
    copies = jnp.broadcast_to(states[None], (n,) + states.shape)
    every = lax.all_to_all(copies, axis, 0, 0, tiled=True)
    return every.reshape(n * states.shape[0], states.shape[1])


def split3(x):
    hi = x.astype(jnp.bfloat16)
    rest = x - hi.astype(jnp.float32)
    mid = rest.astype(jnp.bfloat16)
    lo = (rest - mid.astype(jnp.float32)).astype(jnp.bfloat16)
    return hi, mid, lo


def exact_select(x, onehot):
    hi, mid, lo = split3(x)
    dot = lambda a: jnp.dot(a, onehot, preferred_element_type=jnp.float32)
    return (dot(hi) + dot(mid)) + dot(lo)


def local(states, slot_map, potential, projectors, species, coupling):
    highest = lax.Precision.HIGHEST
    bands = states.shape[0]
    planes = potential.shape[0]
    length = potential.shape[1]
    side = NSIDE
    npw = lax.axis_size(PW)
    stick_count = side * side // npw
    owner = lax.axis_index(PW)
    group = lax.axis_index("band")
    ngroup = lax.axis_size("band")
    every = gathered_bands(states, "band")
    total = every.shape[0]
    count = states.shape[1]
    wide = states.astype(jnp.float32)
    plane_of = slot_map // stick_count
    stick_of = slot_map % stick_count
    on_stick = stick_of[:, None] == jnp.arange(stick_count)[None, :]
    on_plane = jnp.arange(length)[:, None] == plane_of[None, :]
    spread = jnp.where(on_stick[:, None, :], every.T[:, :, None], jnp.zeros((), every.dtype))
    dense = jnp.dot(
        on_plane.astype(jnp.bfloat16),
        spread.reshape(count, total * stick_count),
        preferred_element_type=jnp.float32,
    )
    z_table = cas_table(jnp.arange(length), length)
    side_table = cas_table(side_frequency(jnp.arange(side)), length)
    columns = jnp.dot(z_table.T, dense, precision=highest, preferred_element_type=jnp.float32)
    energies = kinetic(slot_map, owner * stick_count, stick_count, length, side)
    partial_corr = lax.dot_general(
        every, projectors, (((1,), (1,)), ((), ())), preferred_element_type=jnp.float32
    ).T
    partial_kin = lax.dot_general(
        energies[None, :] * wide,
        every.astype(jnp.float32),
        (((1,), (1,)), ((), ())),
        precision=highest,
        preferred_element_type=jnp.float32,
    )
    nproj = partial_corr.shape[0]
    packed = jnp.concatenate([partial_corr.reshape(-1), partial_kin.reshape(-1)])
    width = -(-packed.shape[0] // npw)
    packed = jnp.pad(packed, (0, width * npw - packed.shape[0])).reshape(npw, width)
    sent = jnp.concatenate([columns.reshape(npw, planes * total * stick_count), packed], axis=1)
    got = lax.all_to_all(sent, PW, 0, 0, tiled=True)
    piece = got[:, : planes * total * stick_count].reshape(npw, total, stick_count)
    owned = jnp.sum(got[:, planes * total * stick_count :], axis=0)
    mine = lax.dynamic_slice_in_dim(piece, group * bands, bands, axis=1)
    grid = jnp.transpose(mine, (1, 0, 2)).reshape(bands, planes, side, side)
    half = jnp.einsum("bzjk,jx->bzxk", grid, side_table, precision=highest)
    real_space = jnp.einsum("bzxk,ky->bzxy", half, side_table, precision=highest)
    weighted = real_space * potential[None]
    back_half = jnp.einsum("bzxy,ky->bzxk", weighted, side_table, precision=highest)
    back_grid = jnp.einsum("bzxk,jx->bzjk", back_half, side_table, precision=highest)
    back_own = back_grid.reshape(bands, side * side)
    plane_gram = lax.dot_general(
        back_own,
        jnp.transpose(piece, (1, 0, 2)).reshape(total, side * side),
        (((1,), (1,)), ((), ())),
        precision=highest,
        preferred_element_type=jnp.float32,
    )
    back = jnp.transpose(back_own.reshape(bands, npw, stick_count), (1, 0, 2))
    ret_sent = jnp.concatenate(
        [
            back.reshape(npw, bands * stick_count),
            jnp.broadcast_to(plane_gram.reshape(1, -1), (npw, bands * total)),
            jnp.broadcast_to(owned[None, :], (npw, width)),
        ],
        axis=1,
    )
    ret = lax.all_to_all(ret_sent, PW, 0, 0, tiled=True)
    returned = ret[:, : bands * stick_count].reshape(npw * planes, bands, stick_count)
    gram_local = jnp.sum(
        ret[:, bands * stick_count : bands * stick_count + bands * total], axis=0
    ).reshape(bands, total)
    reduced = ret[:, bands * stick_count + bands * total :].reshape(-1)
    correlations = reduced[: nproj * total].reshape(nproj, total) / math.sqrt(NG)
    gram_kin = reduced[nproj * total : nproj * total + bands * total].reshape(bands, total)
    spectral = jnp.einsum("zbs,kz->bsk", returned, z_table, precision=highest)
    picked = exact_select(
        spectral.reshape(bands * stick_count, length), on_plane.astype(jnp.bfloat16)
    ).reshape(bands, stick_count, -1)
    local_term = jnp.sum(jnp.where(on_stick.T[None], picked, 0.0), axis=1)
    atoms = species.shape[0]
    per_atom = coupling.shape[1]
    kinds = coupling.shape[0]
    symmetric = 0.5 * (coupling + jnp.swapaxes(coupling, 1, 2))
    onehot = (species[:, None] == jnp.arange(kinds)[None, :]).astype(jnp.float32)
    chosen = jnp.einsum("as,smn->amn", onehot, symmetric, precision=highest)
    weights = jnp.einsum(
        "amn,anb->amb", chosen, correlations.reshape(atoms, per_atom, total), precision=highest
    )
    weights = weights.reshape(atoms * per_atom, total).astype(jnp.bfloat16)
    nonlocal_term = lax.dot_general(
        lax.dynamic_slice_in_dim(weights, group * bands, bands, axis=1), projectors, (((0,), (0,)), ((), ())), preferred_element_type=jnp.float32
    ) / math.sqrt(atoms * per_atom)
    applied = energies[None, :] * wide + local_term + nonlocal_term
    cross = lax.dot_general(
        lax.dynamic_slice_in_dim(correlations, group * bands, bands, axis=1),
        weights.astype(jnp.float32),
        (((0,), (0,)), ((), ())),
        precision=highest,
        preferred_element_type=jnp.float32,
    ) / (math.sqrt(atoms * per_atom) * math.sqrt(NG))
    subspace = (gram_kin + gram_local) / float(NG) + cross
    return (applied, subspace)


def solution(mesh):
    split = Mesh(
        mesh.devices.reshape(mesh.shape["band"], 2, 4, 8, 2),
        ("band", "pw_0", "pw_1", "pw_2", "pw_3"),
    )
    return jax.shard_map(
        local,
        mesh=split,
        in_specs=(P("band", PW), P(PW), P(PW, None, None), P(None, PW), P(), P()),
        out_specs=(P("band", PW), P("band", None)),
        check_vma=False,
    )
```

```python
import math

import jax
import jax.numpy as jnp
from jax import lax
from jax.sharding import Mesh
from jax.sharding import PartitionSpec as P

NSIDE = 96
NG = 884736
PW = ("pw_0", "pw_1", "pw_2", "pw_3")


def one_axis_at_a_time(x, axes):
    for a in axes:
        x = lax.psum(x, a)
    return x


def butterfly(x, axes):
    for a in axes:
        n = lax.axis_size(a)
        d = 1
        while d < n:
            x = x + lax.ppermute(x, a, [(i, i ^ d) for i in range(n)])
            d *= 2
    return x


def cas_table(frequency, length):
    columns = jnp.arange(length)
    phases = frequency[:, None] * columns[None, :] % length
    angles = phases.astype(jnp.float32) * (2.0 * math.pi / length)
    return (jnp.cos(angles) + jnp.sin(angles)) / math.sqrt(length)


def side_frequency(indices):
    halves = (indices + 1) // 2
    return jnp.where(indices % 2 == 1, halves, -halves)


def kinetic(slot_map, first_stick, stick_count, length, side):
    sticks = first_stick + slot_map % stick_count
    plane_index = slot_map // stick_count
    along_z = jnp.where(plane_index < length // 2, plane_index, plane_index - length)
    along_x = side_frequency(sticks // side)
    along_y = side_frequency(sticks % side)
    squared = along_x * along_x + along_y * along_y + along_z * along_z
    return squared.astype(jnp.float32) * (1.0 / (0.5 * side * side + 0.25 * length * length))


def gathered_bands(states, axis):
    n = lax.axis_size(axis)
    copies = jnp.broadcast_to(states[None], (n,) + states.shape)
    every = lax.all_to_all(copies, axis, 0, 0, tiled=True)
    return every.reshape(n * states.shape[0], states.shape[1])


def split3(x):
    hi = lax.reduce_precision(x, exponent_bits=8, mantissa_bits=7)
    rest = x - hi
    mid = lax.reduce_precision(rest, exponent_bits=8, mantissa_bits=7)
    lo = rest - mid
    return hi.astype(jnp.bfloat16), mid.astype(jnp.bfloat16), lo.astype(jnp.bfloat16)


def exact_select(x, onehot):
    hi, mid, lo = split3(x)
    dot = lambda a: jnp.dot(a, onehot, preferred_element_type=jnp.float32)
    return (dot(hi) + dot(mid)) + dot(lo)


def local(states, slot_map, potential, projectors, species, coupling):
    highest = lax.Precision.HIGHEST
    bands = states.shape[0]
    planes = potential.shape[0]
    length = potential.shape[1]
    side = NSIDE
    npw = lax.axis_size(PW)
    stick_count = side * side // npw
    owner = lax.axis_index(PW)
    group = lax.axis_index("band")
    ngroup = lax.axis_size("band")
    every = gathered_bands(states, "band")
    total = every.shape[0]
    count = states.shape[1]
    wide = states.astype(jnp.float32)
    plane_of = slot_map // stick_count
    stick_of = slot_map % stick_count
    on_stick = stick_of[:, None] == jnp.arange(stick_count)[None, :]
    on_plane = jnp.arange(length)[:, None] == plane_of[None, :]
    spread = jnp.where(on_stick[:, None, :], every.T[:, :, None], jnp.zeros((), every.dtype))
    dense = jnp.dot(
        on_plane.astype(jnp.bfloat16),
        spread.reshape(count, total * stick_count),
        preferred_element_type=jnp.float32,
    )
    z_table = cas_table(jnp.arange(length), length)
    side_table = cas_table(side_frequency(jnp.arange(side)), length)
    columns = jnp.dot(z_table.T, dense, precision=highest, preferred_element_type=jnp.float32)
    energies = kinetic(slot_map, owner * stick_count, stick_count, length, side)
    partial_corr = lax.dot_general(
        every, projectors, (((1,), (1,)), ((), ())), preferred_element_type=jnp.float32
    ).T
    partial_kin = lax.dot_general(
        energies[None, :] * wide,
        every.astype(jnp.float32),
        (((1,), (1,)), ((), ())),
        precision=highest,
        preferred_element_type=jnp.float32,
    )
    nproj = partial_corr.shape[0]
    packed = jnp.concatenate([partial_corr.reshape(-1), partial_kin.reshape(-1)])
    width = -(-packed.shape[0] // npw)
    packed = jnp.pad(packed, (0, width * npw - packed.shape[0])).reshape(npw, width)
    sent = jnp.concatenate([columns.reshape(npw, planes * total * stick_count), packed], axis=1)
    got = lax.all_to_all(sent, PW, 0, 0, tiled=True)
    piece = got[:, : planes * total * stick_count].reshape(npw, total, stick_count)
    owned = jnp.sum(got[:, planes * total * stick_count :], axis=0)
    mine = lax.dynamic_slice_in_dim(piece, group * bands, bands, axis=1)
    grid = jnp.transpose(mine, (1, 0, 2)).reshape(bands, planes, side, side)
    half = jnp.einsum("bzjk,jx->bzxk", grid, side_table, precision=highest)
    real_space = jnp.einsum("bzxk,ky->bzxy", half, side_table, precision=highest)
    weighted = real_space * potential[None]
    back_half = jnp.einsum("bzxy,ky->bzxk", weighted, side_table, precision=highest)
    back_grid = jnp.einsum("bzxk,jx->bzjk", back_half, side_table, precision=highest)
    back_own = back_grid.reshape(bands, side * side)
    plane_gram = lax.dot_general(
        back_own,
        jnp.transpose(piece, (1, 0, 2)).reshape(total, side * side),
        (((1,), (1,)), ((), ())),
        precision=highest,
        preferred_element_type=jnp.float32,
    )
    back = jnp.transpose(back_own.reshape(bands, npw, stick_count), (1, 0, 2))
    ret_sent = jnp.concatenate(
        [
            back.reshape(npw, bands * stick_count),
            jnp.broadcast_to(plane_gram.reshape(1, -1), (npw, bands * total)),
            jnp.broadcast_to(owned[None, :], (npw, width)),
        ],
        axis=1,
    )
    ret = lax.all_to_all(ret_sent, PW, 0, 0, tiled=True)
    returned = ret[:, : bands * stick_count].reshape(npw * planes, bands, stick_count)
    gram_local = jnp.sum(
        ret[:, bands * stick_count : bands * stick_count + bands * total], axis=0
    ).reshape(bands, total)
    reduced = ret[:, bands * stick_count + bands * total :].reshape(-1)
    correlations = reduced[: nproj * total].reshape(nproj, total) / math.sqrt(NG)
    gram_kin = reduced[nproj * total : nproj * total + bands * total].reshape(bands, total)
    spectral = jnp.einsum("zbs,kz->bsk", returned, z_table, precision=highest)
    picked = exact_select(
        spectral.reshape(bands * stick_count, length), on_plane.astype(jnp.bfloat16)
    ).reshape(bands, stick_count, -1)
    local_term = jnp.sum(jnp.where(on_stick.T[None], picked, 0.0), axis=1)
    atoms = species.shape[0]
    per_atom = coupling.shape[1]
    kinds = coupling.shape[0]
    symmetric = 0.5 * (coupling + jnp.swapaxes(coupling, 1, 2))
    onehot = (species[:, None] == jnp.arange(kinds)[None, :]).astype(jnp.float32)
    chosen = jnp.einsum("as,smn->amn", onehot, symmetric, precision=highest)
    weights = jnp.einsum(
        "amn,anb->amb", chosen, correlations.reshape(atoms, per_atom, total), precision=highest
    )
    weights = weights.reshape(atoms * per_atom, total).astype(jnp.bfloat16)
    nonlocal_term = lax.dot_general(
        lax.dynamic_slice_in_dim(weights, group * bands, bands, axis=1), projectors, (((0,), (0,)), ((), ())), preferred_element_type=jnp.float32
    ) / math.sqrt(atoms * per_atom)
    applied = energies[None, :] * wide + local_term + nonlocal_term
    cross = lax.dot_general(
        lax.dynamic_slice_in_dim(correlations, group * bands, bands, axis=1),
        weights.astype(jnp.float32),
        (((0,), (0,)), ((), ())),
        precision=highest,
        preferred_element_type=jnp.float32,
    ) / (math.sqrt(atoms * per_atom) * math.sqrt(NG))
    subspace = (gram_kin + gram_local) / float(NG) + cross
    return (applied, subspace)


def solution(mesh):
    split = Mesh(
        mesh.devices.reshape(mesh.shape["band"], 2, 4, 8, 2),
        ("band", "pw_0", "pw_1", "pw_2", "pw_3"),
    )
    return jax.shard_map(
        local,
        mesh=split,
        in_specs=(P("band", PW), P(PW), P(PW, None, None), P(None, PW), P(), P()),
        out_specs=(P("band", PW), P("band", None)),
        check_vma=False,
    )
```

```python
import math

import jax
import jax.numpy as jnp
from jax import lax
from jax.sharding import Mesh
from jax.sharding import PartitionSpec as P

NSIDE = 96
NG = 884736
PW = ("pw_0", "pw_1", "pw_2", "pw_3")


def one_axis_at_a_time(x, axes):
    for a in axes:
        x = lax.psum(x, a)
    return x


def butterfly(x, axes):
    for a in axes:
        n = lax.axis_size(a)
        d = 1
        while d < n:
            x = x + lax.ppermute(x, a, [(i, i ^ d) for i in range(n)])
            d *= 2
    return x


def cas_table(frequency, length):
    columns = jnp.arange(length)
    phases = frequency[:, None] * columns[None, :] % length
    angles = phases.astype(jnp.float32) * (2.0 * math.pi / length)
    return (jnp.cos(angles) + jnp.sin(angles)) / math.sqrt(length)


def side_frequency(indices):
    halves = (indices + 1) // 2
    return jnp.where(indices % 2 == 1, halves, -halves)


def kinetic(slot_map, first_stick, stick_count, length, side):
    sticks = first_stick + slot_map % stick_count
    plane_index = slot_map // stick_count
    along_z = jnp.where(plane_index < length // 2, plane_index, plane_index - length)
    along_x = side_frequency(sticks // side)
    along_y = side_frequency(sticks % side)
    squared = along_x * along_x + along_y * along_y + along_z * along_z
    return squared.astype(jnp.float32) * (1.0 / (0.5 * side * side + 0.25 * length * length))


def gathered_bands(states, axis):
    n = lax.axis_size(axis)
    copies = jnp.broadcast_to(states[None], (n,) + states.shape)
    every = lax.all_to_all(copies, axis, 0, 0, tiled=True)
    return every.reshape(n * states.shape[0], states.shape[1])


def split3(x):
    hi = lax.reduce_precision(x, exponent_bits=8, mantissa_bits=7)
    rest = x - hi
    mid = lax.reduce_precision(rest, exponent_bits=8, mantissa_bits=7)
    lo = rest - mid
    return hi.astype(jnp.bfloat16), mid.astype(jnp.bfloat16), lo.astype(jnp.bfloat16)


def split2(x):
    hi = lax.reduce_precision(x, exponent_bits=8, mantissa_bits=7)
    return hi.astype(jnp.bfloat16), (x - hi).astype(jnp.bfloat16)


def exact_select(x, onehot):
    hi, mid, lo = split3(x)
    dot = lambda a: jnp.dot(a, onehot, preferred_element_type=jnp.float32)
    return (dot(hi) + dot(mid)) + dot(lo)


def local(states, slot_map, potential, projectors, species, coupling):
    highest = lax.Precision.HIGHEST
    bands = states.shape[0]
    planes = potential.shape[0]
    length = potential.shape[1]
    side = NSIDE
    npw = lax.axis_size(PW)
    stick_count = side * side // npw
    owner = lax.axis_index(PW)
    group = lax.axis_index("band")
    ngroup = lax.axis_size("band")
    every = gathered_bands(states, "band")
    total = every.shape[0]
    count = states.shape[1]
    wide = states.astype(jnp.float32)
    plane_of = slot_map // stick_count
    stick_of = slot_map % stick_count
    on_stick = stick_of[:, None] == jnp.arange(stick_count)[None, :]
    on_plane = jnp.arange(length)[:, None] == plane_of[None, :]
    spread = jnp.where(on_stick[:, None, :], every.T[:, :, None], jnp.zeros((), every.dtype))
    dense = jnp.dot(
        on_plane.astype(jnp.bfloat16),
        spread.reshape(count, total * stick_count),
        preferred_element_type=jnp.float32,
    )
    z_table = cas_table(jnp.arange(length), length)
    side_table = cas_table(side_frequency(jnp.arange(side)), length)
    columns = jnp.dot(z_table.T, dense, precision=highest, preferred_element_type=jnp.float32)
    energies = kinetic(slot_map, owner * stick_count, stick_count, length, side)
    partial_corr = lax.dot_general(
        every, projectors, (((1,), (1,)), ((), ())), preferred_element_type=jnp.float32
    ).T
    partial_kin = lax.dot_general(
        energies[None, :] * wide,
        every.astype(jnp.float32),
        (((1,), (1,)), ((), ())),
        precision=highest,
        preferred_element_type=jnp.float32,
    )
    nproj = partial_corr.shape[0]
    packed = jnp.concatenate([partial_corr.reshape(-1), partial_kin.reshape(-1)])
    width = -(-packed.shape[0] // npw)
    packed = jnp.pad(packed, (0, width * npw - packed.shape[0])).reshape(npw, width)
    columns = columns.reshape(npw, total, stick_count)
    exact = jnp.concatenate(
        [lax.dynamic_slice_in_dim(columns, group * bands, bands, axis=1).reshape(npw, -1), packed], axis=1
    )
    exact_hi, exact_lo = split2(exact)
    sent = jnp.concatenate(
        [exact_hi, exact_lo, columns.reshape(npw, -1).astype(jnp.bfloat16)], axis=1
    )
    got = lax.all_to_all(sent, PW, 0, 0, tiled=True)
    nexact = exact.shape[1]
    joined = got[:, :nexact].astype(jnp.float32) + got[:, nexact : 2 * nexact].astype(jnp.float32)
    mine = joined[:, : bands * stick_count].reshape(npw, bands, stick_count)
    owned = jnp.sum(joined[:, bands * stick_count :], axis=0)
    piece = got[:, 2 * nexact :].astype(jnp.float32).reshape(npw, total, stick_count)
    grid = jnp.transpose(mine, (1, 0, 2)).reshape(bands, planes, side, side)
    half = jnp.einsum("bzjk,jx->bzxk", grid, side_table, precision=highest)
    real_space = jnp.einsum("bzxk,ky->bzxy", half, side_table, precision=highest)
    weighted = real_space * potential[None]
    back_half = jnp.einsum("bzxy,ky->bzxk", weighted, side_table, precision=highest)
    back_grid = jnp.einsum("bzxk,jx->bzjk", back_half, side_table, precision=highest)
    back_own = back_grid.reshape(bands, side * side)
    piece = lax.dynamic_update_slice_in_dim(piece, mine, group * bands, axis=1)
    plane_gram = lax.dot_general(
        back_own,
        jnp.transpose(piece, (1, 0, 2)).reshape(total, side * side),
        (((1,), (1,)), ((), ())),
        precision=highest,
        preferred_element_type=jnp.float32,
    )
    back = jnp.transpose(back_own.reshape(bands, npw, stick_count), (1, 0, 2))
    ret_sent = jnp.concatenate(
        [
            back.reshape(npw, bands * stick_count),
            jnp.broadcast_to(plane_gram.reshape(1, -1), (npw, bands * total)),
            jnp.broadcast_to(owned[None, :], (npw, width)),
        ],
        axis=1,
    )
    ret = lax.all_to_all(ret_sent, PW, 0, 0, tiled=True)
    returned = ret[:, : bands * stick_count].reshape(npw * planes, bands, stick_count)
    gram_local = jnp.sum(
        ret[:, bands * stick_count : bands * stick_count + bands * total], axis=0
    ).reshape(bands, total)
    reduced = ret[:, bands * stick_count + bands * total :].reshape(-1)
    correlations = reduced[: nproj * total].reshape(nproj, total) / math.sqrt(NG)
    gram_kin = reduced[nproj * total : nproj * total + bands * total].reshape(bands, total)
    spectral = jnp.einsum("zbs,kz->bsk", returned, z_table, precision=highest)
    picked = exact_select(
        spectral.reshape(bands * stick_count, length), on_plane.astype(jnp.bfloat16)
    ).reshape(bands, stick_count, -1)
    local_term = jnp.sum(jnp.where(on_stick.T[None], picked, 0.0), axis=1)
    atoms = species.shape[0]
    per_atom = coupling.shape[1]
    kinds = coupling.shape[0]
    symmetric = 0.5 * (coupling + jnp.swapaxes(coupling, 1, 2))
    onehot = (species[:, None] == jnp.arange(kinds)[None, :]).astype(jnp.float32)
    chosen = jnp.einsum("as,smn->amn", onehot, symmetric, precision=highest)
    weights = jnp.einsum(
        "amn,anb->amb", chosen, correlations.reshape(atoms, per_atom, total), precision=highest
    )
    weights = weights.reshape(atoms * per_atom, total).astype(jnp.bfloat16)
    nonlocal_term = lax.dot_general(
        lax.dynamic_slice_in_dim(weights, group * bands, bands, axis=1), projectors, (((0,), (0,)), ((), ())), preferred_element_type=jnp.float32
    ) / math.sqrt(atoms * per_atom)
    applied = energies[None, :] * wide + local_term + nonlocal_term
    cross = lax.dot_general(
        lax.dynamic_slice_in_dim(correlations, group * bands, bands, axis=1),
        weights.astype(jnp.float32),
        (((0,), (0,)), ((), ())),
        precision=highest,
        preferred_element_type=jnp.float32,
    ) / (math.sqrt(atoms * per_atom) * math.sqrt(NG))
    subspace = (gram_kin + gram_local) / float(NG) + cross
    return (applied, subspace)


def solution(mesh):
    split = Mesh(
        mesh.devices.reshape(mesh.shape["band"], 2, 4, 8, 2),
        ("band", "pw_0", "pw_1", "pw_2", "pw_3"),
    )
    return jax.shard_map(
        local,
        mesh=split,
        in_specs=(P("band", PW), P(PW), P(PW, None, None), P(None, PW), P(), P()),
        out_specs=(P("band", PW), P("band", None)),
        check_vma=False,
    )
```

```python
import math

import jax
import jax.numpy as jnp
from jax import lax
from jax.sharding import Mesh
from jax.sharding import PartitionSpec as P

NSIDE = 96
NG = 884736
PW = ("pw_0", "pw_1", "pw_2", "pw_3")


def one_axis_at_a_time(x, axes):
    for a in axes:
        x = lax.psum(x, a)
    return x


def butterfly(x, axes):
    for a in axes:
        n = lax.axis_size(a)
        d = 1
        while d < n:
            x = x + lax.ppermute(x, a, [(i, i ^ d) for i in range(n)])
            d *= 2
    return x


def cas_table(frequency, length):
    columns = jnp.arange(length)
    phases = frequency[:, None] * columns[None, :] % length
    angles = phases.astype(jnp.float32) * (2.0 * math.pi / length)
    return (jnp.cos(angles) + jnp.sin(angles)) / math.sqrt(length)


def side_frequency(indices):
    halves = (indices + 1) // 2
    return jnp.where(indices % 2 == 1, halves, -halves)


def kinetic(slot_map, first_stick, stick_count, length, side):
    sticks = first_stick + slot_map % stick_count
    plane_index = slot_map // stick_count
    along_z = jnp.where(plane_index < length // 2, plane_index, plane_index - length)
    along_x = side_frequency(sticks // side)
    along_y = side_frequency(sticks % side)
    squared = along_x * along_x + along_y * along_y + along_z * along_z
    return squared.astype(jnp.float32) * (1.0 / (0.5 * side * side + 0.25 * length * length))


def gathered_bands(states, axis):
    n = lax.axis_size(axis)
    copies = jnp.broadcast_to(states[None], (n,) + states.shape)
    every = lax.all_to_all(copies, axis, 0, 0, tiled=True)
    return every.reshape(n * states.shape[0], states.shape[1])


def split3(x):
    hi = lax.reduce_precision(x, exponent_bits=8, mantissa_bits=7)
    rest = x - hi
    mid = lax.reduce_precision(rest, exponent_bits=8, mantissa_bits=7)
    lo = rest - mid
    return hi.astype(jnp.bfloat16), mid.astype(jnp.bfloat16), lo.astype(jnp.bfloat16)


def split2(x):
    hi = lax.reduce_precision(x, exponent_bits=8, mantissa_bits=7)
    return hi.astype(jnp.bfloat16), (x - hi).astype(jnp.bfloat16)


def exact_select(x, onehot):
    hi, mid, lo = split3(x)
    dot = lambda a: jnp.dot(a, onehot, preferred_element_type=jnp.float32)
    return (dot(hi) + dot(mid)) + dot(lo)


def local(states, slot_map, potential, projectors, species, coupling):
    highest = lax.Precision.HIGHEST
    bands = states.shape[0]
    planes = potential.shape[0]
    length = potential.shape[1]
    side = NSIDE
    npw = lax.axis_size(PW)
    stick_count = side * side // npw
    owner = lax.axis_index(PW)
    group = lax.axis_index("band")
    ngroup = lax.axis_size("band")
    every = gathered_bands(states, "band")
    total = every.shape[0]
    count = states.shape[1]
    wide = states.astype(jnp.float32)
    plane_of = slot_map // stick_count
    stick_of = slot_map % stick_count
    on_stick = stick_of[:, None] == jnp.arange(stick_count)[None, :]
    on_plane = jnp.arange(length)[:, None] == plane_of[None, :]
    spread = jnp.where(on_stick[:, None, :], every.T[:, :, None], jnp.zeros((), every.dtype))
    dense = jnp.dot(
        on_plane.astype(jnp.bfloat16),
        spread.reshape(count, total * stick_count),
        preferred_element_type=jnp.float32,
    )
    z_table = cas_table(jnp.arange(length), length)
    side_table = cas_table(side_frequency(jnp.arange(side)), length)
    columns = jnp.dot(z_table.T, dense, precision=highest, preferred_element_type=jnp.float32)
    energies = kinetic(slot_map, owner * stick_count, stick_count, length, side)
    partial_corr = lax.dot_general(
        every, projectors, (((1,), (1,)), ((), ())), preferred_element_type=jnp.float32
    ).T
    partial_kin = lax.dot_general(
        energies[None, :] * wide,
        every.astype(jnp.float32),
        (((1,), (1,)), ((), ())),
        precision=highest,
        preferred_element_type=jnp.float32,
    )
    nproj = partial_corr.shape[0]
    packed = jnp.concatenate([partial_corr.reshape(-1), partial_kin.reshape(-1)])
    width = -(-packed.shape[0] // npw)
    packed = jnp.pad(packed, (0, width * npw - packed.shape[0])).reshape(npw, width)
    columns = columns.reshape(npw, total, stick_count)
    columns_hi = lax.reduce_precision(columns, exponent_bits=8, mantissa_bits=7)
    columns_lo = lax.dynamic_slice_in_dim(columns - columns_hi, group * bands, bands, axis=1)
    packed_hi, packed_lo = split2(packed)
    sent = jnp.concatenate(
        [
            columns_hi.reshape(npw, -1).astype(jnp.bfloat16),
            columns_lo.reshape(npw, -1).astype(jnp.bfloat16),
            packed_hi,
            packed_lo,
        ],
        axis=1,
    )
    got = lax.all_to_all(sent, PW, 0, 0, tiled=True)
    nall = total * stick_count
    nown = bands * stick_count
    piece = got[:, :nall].astype(jnp.float32).reshape(npw, total, stick_count)
    mine = lax.dynamic_slice_in_dim(piece, group * bands, bands, axis=1) + got[
        :, nall : nall + nown
    ].astype(jnp.float32).reshape(npw, bands, stick_count)
    owned = jnp.sum(
        got[:, nall + nown : nall + nown + width].astype(jnp.float32)
        + got[:, nall + nown + width :].astype(jnp.float32),
        axis=0,
    )
    grid = jnp.transpose(mine, (1, 0, 2)).reshape(bands, planes, side, side)
    half = jnp.einsum("bzjk,jx->bzxk", grid, side_table, precision=highest)
    real_space = jnp.einsum("bzxk,ky->bzxy", half, side_table, precision=highest)
    weighted = real_space * potential[None]
    back_half = jnp.einsum("bzxy,ky->bzxk", weighted, side_table, precision=highest)
    back_grid = jnp.einsum("bzxk,jx->bzjk", back_half, side_table, precision=highest)
    back_own = back_grid.reshape(bands, side * side)
    piece = lax.dynamic_update_slice_in_dim(piece, mine, group * bands, axis=1)
    plane_gram = lax.dot_general(
        back_own,
        jnp.transpose(piece, (1, 0, 2)).reshape(total, side * side),
        (((1,), (1,)), ((), ())),
        precision=highest,
        preferred_element_type=jnp.float32,
    )
    back = jnp.transpose(back_own.reshape(bands, npw, stick_count), (1, 0, 2))
    ret_sent = jnp.concatenate(
        [
            back.reshape(npw, bands * stick_count),
            jnp.broadcast_to(plane_gram.reshape(1, -1), (npw, bands * total)),
            jnp.broadcast_to(owned[None, :], (npw, width)),
        ],
        axis=1,
    )
    ret = lax.all_to_all(ret_sent, PW, 0, 0, tiled=True)
    returned = ret[:, : bands * stick_count].reshape(npw * planes, bands, stick_count)
    gram_local = jnp.sum(
        ret[:, bands * stick_count : bands * stick_count + bands * total], axis=0
    ).reshape(bands, total)
    reduced = ret[:, bands * stick_count + bands * total :].reshape(-1)
    correlations = reduced[: nproj * total].reshape(nproj, total) / math.sqrt(NG)
    gram_kin = reduced[nproj * total : nproj * total + bands * total].reshape(bands, total)
    spectral = jnp.einsum("zbs,kz->bsk", returned, z_table, precision=highest)
    picked = exact_select(
        spectral.reshape(bands * stick_count, length), on_plane.astype(jnp.bfloat16)
    ).reshape(bands, stick_count, -1)
    local_term = jnp.sum(jnp.where(on_stick.T[None], picked, 0.0), axis=1)
    atoms = species.shape[0]
    per_atom = coupling.shape[1]
    kinds = coupling.shape[0]
    symmetric = 0.5 * (coupling + jnp.swapaxes(coupling, 1, 2))
    onehot = (species[:, None] == jnp.arange(kinds)[None, :]).astype(jnp.float32)
    chosen = jnp.einsum("as,smn->amn", onehot, symmetric, precision=highest)
    weights = jnp.einsum(
        "amn,anb->amb", chosen, correlations.reshape(atoms, per_atom, total), precision=highest
    )
    weights = weights.reshape(atoms * per_atom, total).astype(jnp.bfloat16)
    nonlocal_term = lax.dot_general(
        lax.dynamic_slice_in_dim(weights, group * bands, bands, axis=1), projectors, (((0,), (0,)), ((), ())), preferred_element_type=jnp.float32
    ) / math.sqrt(atoms * per_atom)
    applied = energies[None, :] * wide + local_term + nonlocal_term
    cross = lax.dot_general(
        lax.dynamic_slice_in_dim(correlations, group * bands, bands, axis=1),
        weights.astype(jnp.float32),
        (((0,), (0,)), ((), ())),
        precision=highest,
        preferred_element_type=jnp.float32,
    ) / (math.sqrt(atoms * per_atom) * math.sqrt(NG))
    subspace = (gram_kin + gram_local) / float(NG) + cross
    return (applied, subspace)


def solution(mesh):
    split = Mesh(
        mesh.devices.reshape(mesh.shape["band"], 2, 4, 8, 2),
        ("band", "pw_0", "pw_1", "pw_2", "pw_3"),
    )
    return jax.shard_map(
        local,
        mesh=split,
        in_specs=(P("band", PW), P(PW), P(PW, None, None), P(None, PW), P(), P()),
        out_specs=(P("band", PW), P("band", None)),
        check_vma=False,
    )
```

```python
import math

import jax
import jax.numpy as jnp
from jax import lax
from jax.sharding import Mesh
from jax.sharding import PartitionSpec as P

NSIDE = 96
NG = 884736
PW = ("pw_0", "pw_1", "pw_2", "pw_3")


def one_axis_at_a_time(x, axes):
    for a in axes:
        x = lax.psum(x, a)
    return x


def butterfly(x, axes):
    for a in axes:
        n = lax.axis_size(a)
        d = 1
        while d < n:
            x = x + lax.ppermute(x, a, [(i, i ^ d) for i in range(n)])
            d *= 2
    return x


def cas_table(frequency, length):
    columns = jnp.arange(length)
    phases = frequency[:, None] * columns[None, :] % length
    angles = phases.astype(jnp.float32) * (2.0 * math.pi / length)
    return (jnp.cos(angles) + jnp.sin(angles)) / math.sqrt(length)


def side_frequency(indices):
    halves = (indices + 1) // 2
    return jnp.where(indices % 2 == 1, halves, -halves)


def kinetic(slot_map, first_stick, stick_count, length, side):
    sticks = first_stick + slot_map % stick_count
    plane_index = slot_map // stick_count
    along_z = jnp.where(plane_index < length // 2, plane_index, plane_index - length)
    along_x = side_frequency(sticks // side)
    along_y = side_frequency(sticks % side)
    squared = along_x * along_x + along_y * along_y + along_z * along_z
    return squared.astype(jnp.float32) * (1.0 / (0.5 * side * side + 0.25 * length * length))


def gathered_bands(states, axis):
    n = lax.axis_size(axis)
    copies = jnp.broadcast_to(states[None], (n,) + states.shape)
    every = lax.all_to_all(copies, axis, 0, 0, tiled=True)
    return every.reshape(n * states.shape[0], states.shape[1])


def split3(x):
    hi = lax.reduce_precision(x, exponent_bits=8, mantissa_bits=7)
    rest = x - hi
    mid = lax.reduce_precision(rest, exponent_bits=8, mantissa_bits=7)
    lo = rest - mid
    return hi.astype(jnp.bfloat16), mid.astype(jnp.bfloat16), lo.astype(jnp.bfloat16)


def split2(x):
    hi = lax.reduce_precision(x, exponent_bits=8, mantissa_bits=7)
    return hi.astype(jnp.bfloat16), (x - hi).astype(jnp.bfloat16)


def exact_select(x, onehot):
    hi, mid, lo = split3(x)
    dot = lambda a: jnp.dot(a, onehot, preferred_element_type=jnp.float32)
    return (dot(hi) + dot(mid)) + dot(lo)


def local(states, slot_map, potential, projectors, species, coupling):
    highest = lax.Precision.HIGHEST
    bands = states.shape[0]
    planes = potential.shape[0]
    length = potential.shape[1]
    side = NSIDE
    npw = lax.axis_size(PW)
    stick_count = side * side // npw
    owner = lax.axis_index(PW)
    group = lax.axis_index("band")
    ngroup = lax.axis_size("band")
    every = gathered_bands(states, "band")
    total = every.shape[0]
    count = states.shape[1]
    wide = states.astype(jnp.float32)
    plane_of = slot_map // stick_count
    stick_of = slot_map % stick_count
    on_stick = stick_of[:, None] == jnp.arange(stick_count)[None, :]
    on_plane = jnp.arange(length)[:, None] == plane_of[None, :]
    spread = jnp.where(on_stick[:, None, :], every.T[:, :, None], jnp.zeros((), every.dtype))
    dense = jnp.dot(
        on_plane.astype(jnp.bfloat16),
        spread.reshape(count, total * stick_count),
        preferred_element_type=jnp.float32,
    )
    z_table = cas_table(jnp.arange(length), length)
    side_table = cas_table(side_frequency(jnp.arange(side)), length)
    columns = jnp.dot(z_table.T, dense, precision=highest, preferred_element_type=jnp.float32)
    energies = kinetic(slot_map, owner * stick_count, stick_count, length, side)
    lanes = -(-total // 128) * 128
    partial_corr = lax.dot_general(
        projectors,
        jnp.pad(every, ((0, lanes - total), (0, 0))),
        (((1,), (1,)), ((), ())),
        preferred_element_type=jnp.float32,
    )[:, :total]
    partial_kin = lax.dot_general(
        energies[None, :] * wide,
        every.astype(jnp.float32),
        (((1,), (1,)), ((), ())),
        precision=highest,
        preferred_element_type=jnp.float32,
    )
    nproj = partial_corr.shape[0]
    packed = jnp.concatenate([partial_corr.reshape(-1), partial_kin.reshape(-1)])
    width = -(-packed.shape[0] // npw)
    packed = jnp.pad(packed, (0, width * npw - packed.shape[0])).reshape(npw, width)
    columns = columns.reshape(npw, total, stick_count)
    columns_hi = lax.reduce_precision(columns, exponent_bits=8, mantissa_bits=7)
    columns_lo = lax.dynamic_slice_in_dim(columns - columns_hi, group * bands, bands, axis=1)
    packed_hi, packed_lo = split2(packed)
    sent = jnp.concatenate(
        [
            columns_hi.reshape(npw, -1).astype(jnp.bfloat16),
            columns_lo.reshape(npw, -1).astype(jnp.bfloat16),
            packed_hi,
            packed_lo,
        ],
        axis=1,
    )
    got = lax.all_to_all(sent, PW, 0, 0, tiled=True)
    nall = total * stick_count
    nown = bands * stick_count
    piece = got[:, :nall].astype(jnp.float32).reshape(npw, total, stick_count)
    mine = lax.dynamic_slice_in_dim(piece, group * bands, bands, axis=1) + got[
        :, nall : nall + nown
    ].astype(jnp.float32).reshape(npw, bands, stick_count)
    owned = jnp.sum(
        got[:, nall + nown : nall + nown + width].astype(jnp.float32)
        + got[:, nall + nown + width :].astype(jnp.float32),
        axis=0,
    )
    grid = jnp.transpose(mine, (1, 0, 2)).reshape(bands, planes, side, side)
    half = jnp.einsum("bzjk,jx->bzxk", grid, side_table, precision=highest)
    real_space = jnp.einsum("bzxk,ky->bzxy", half, side_table, precision=highest)
    weighted = real_space * potential[None]
    back_half = jnp.einsum("bzxy,ky->bzxk", weighted, side_table, precision=highest)
    back_grid = jnp.einsum("bzxk,jx->bzjk", back_half, side_table, precision=highest)
    back_own = back_grid.reshape(bands, side * side)
    piece = lax.dynamic_update_slice_in_dim(piece, mine, group * bands, axis=1)
    plane_gram = lax.dot_general(
        back_own,
        jnp.transpose(piece, (1, 0, 2)).reshape(total, side * side),
        (((1,), (1,)), ((), ())),
        precision=highest,
        preferred_element_type=jnp.float32,
    )
    back = jnp.transpose(back_own.reshape(bands, npw, stick_count), (1, 0, 2))
    ret_sent = jnp.concatenate(
        [
            back.reshape(npw, bands * stick_count),
            jnp.broadcast_to(plane_gram.reshape(1, -1), (npw, bands * total)),
            jnp.broadcast_to(owned[None, :], (npw, width)),
        ],
        axis=1,
    )
    ret = lax.all_to_all(ret_sent, PW, 0, 0, tiled=True)
    returned = ret[:, : bands * stick_count].reshape(npw * planes, bands, stick_count)
    gram_local = jnp.sum(
        ret[:, bands * stick_count : bands * stick_count + bands * total], axis=0
    ).reshape(bands, total)
    reduced = ret[:, bands * stick_count + bands * total :].reshape(-1)
    correlations = reduced[: nproj * total].reshape(nproj, total) / math.sqrt(NG)
    gram_kin = reduced[nproj * total : nproj * total + bands * total].reshape(bands, total)
    spectral = jnp.einsum("zbs,kz->bsk", returned, z_table, precision=highest)
    picked = exact_select(
        spectral.reshape(bands * stick_count, length), on_plane.astype(jnp.bfloat16)
    ).reshape(bands, stick_count, -1)
    local_term = jnp.sum(jnp.where(on_stick.T[None], picked, 0.0), axis=1)
    atoms = species.shape[0]
    per_atom = coupling.shape[1]
    kinds = coupling.shape[0]
    symmetric = 0.5 * (coupling + jnp.swapaxes(coupling, 1, 2))
    onehot = (species[:, None] == jnp.arange(kinds)[None, :]).astype(jnp.float32)
    chosen = jnp.einsum("as,smn->amn", onehot, symmetric, precision=highest)
    weights = jnp.einsum(
        "amn,anb->amb", chosen, correlations.reshape(atoms, per_atom, total), precision=highest
    )
    weights = weights.reshape(atoms * per_atom, total).astype(jnp.bfloat16)
    nonlocal_term = lax.dot_general(
        lax.dynamic_slice_in_dim(weights, group * bands, bands, axis=1), projectors, (((0,), (0,)), ((), ())), preferred_element_type=jnp.float32
    ) / math.sqrt(atoms * per_atom)
    applied = energies[None, :] * wide + local_term + nonlocal_term
    cross = lax.dot_general(
        lax.dynamic_slice_in_dim(correlations, group * bands, bands, axis=1),
        weights.astype(jnp.float32),
        (((0,), (0,)), ((), ())),
        precision=highest,
        preferred_element_type=jnp.float32,
    ) / (math.sqrt(atoms * per_atom) * math.sqrt(NG))
    subspace = (gram_kin + gram_local) / float(NG) + cross
    return (applied, subspace)


def solution(mesh):
    split = Mesh(
        mesh.devices.reshape(mesh.shape["band"], 2, 4, 8, 2),
        ("band", "pw_0", "pw_1", "pw_2", "pw_3"),
    )
    return jax.shard_map(
        local,
        mesh=split,
        in_specs=(P("band", PW), P(PW), P(PW, None, None), P(None, PW), P(), P()),
        out_specs=(P("band", PW), P("band", None)),
        check_vma=False,
    )
```

```python
import math

import jax
import jax.numpy as jnp
from jax import lax
from jax.sharding import Mesh
from jax.sharding import PartitionSpec as P

NSIDE = 96
NG = 884736
PW = ("pw_0", "pw_1", "pw_2", "pw_3")


def one_axis_at_a_time(x, axes):
    for a in axes:
        x = lax.psum(x, a)
    return x


def butterfly(x, axes):
    for a in axes:
        n = lax.axis_size(a)
        d = 1
        while d < n:
            x = x + lax.ppermute(x, a, [(i, i ^ d) for i in range(n)])
            d *= 2
    return x


def cas_table(frequency, length):
    columns = jnp.arange(length)
    phases = frequency[:, None] * columns[None, :] % length
    angles = phases.astype(jnp.float32) * (2.0 * math.pi / length)
    return (jnp.cos(angles) + jnp.sin(angles)) / math.sqrt(length)


def side_frequency(indices):
    halves = (indices + 1) // 2
    return jnp.where(indices % 2 == 1, halves, -halves)


def kinetic(slot_map, first_stick, stick_count, length, side):
    sticks = first_stick + slot_map % stick_count
    plane_index = slot_map // stick_count
    along_z = jnp.where(plane_index < length // 2, plane_index, plane_index - length)
    along_x = side_frequency(sticks // side)
    along_y = side_frequency(sticks % side)
    squared = along_x * along_x + along_y * along_y + along_z * along_z
    return squared.astype(jnp.float32) * (1.0 / (0.5 * side * side + 0.25 * length * length))


def gathered_bands(states, axis):
    n = lax.axis_size(axis)
    copies = jnp.broadcast_to(states[None], (n,) + states.shape)
    every = lax.all_to_all(copies, axis, 0, 0, tiled=True)
    return every.reshape(n * states.shape[0], states.shape[1])


def split3(x):
    hi = lax.reduce_precision(x, exponent_bits=8, mantissa_bits=7)
    rest = x - hi
    mid = lax.reduce_precision(rest, exponent_bits=8, mantissa_bits=7)
    lo = rest - mid
    return hi.astype(jnp.bfloat16), mid.astype(jnp.bfloat16), lo.astype(jnp.bfloat16)


def split2(x):
    hi = lax.reduce_precision(x, exponent_bits=8, mantissa_bits=7)
    return hi.astype(jnp.bfloat16), (x - hi).astype(jnp.bfloat16)


def exact_select(x, onehot):
    hi, lo = split2(x)
    dot = lambda a: jnp.dot(a, onehot, preferred_element_type=jnp.float32)
    return dot(hi) + dot(lo)


def local(states, slot_map, potential, projectors, species, coupling):
    highest = lax.Precision.HIGHEST
    bands = states.shape[0]
    planes = potential.shape[0]
    length = potential.shape[1]
    side = NSIDE
    npw = lax.axis_size(PW)
    stick_count = side * side // npw
    owner = lax.axis_index(PW)
    group = lax.axis_index("band")
    ngroup = lax.axis_size("band")
    every = gathered_bands(states, "band")
    total = every.shape[0]
    count = states.shape[1]
    wide = states.astype(jnp.float32)
    plane_of = slot_map // stick_count
    stick_of = slot_map % stick_count
    on_stick = stick_of[:, None] == jnp.arange(stick_count)[None, :]
    on_plane = jnp.arange(length)[:, None] == plane_of[None, :]
    spread = jnp.where(on_stick[:, None, :], every.T[:, :, None], jnp.zeros((), every.dtype))
    dense = jnp.dot(
        on_plane.astype(jnp.bfloat16),
        spread.reshape(count, total * stick_count),
        preferred_element_type=jnp.float32,
    )
    z_table = cas_table(jnp.arange(length), length)
    side_table = cas_table(side_frequency(jnp.arange(side)), length)
    columns = jnp.dot(z_table.T, dense, precision=highest, preferred_element_type=jnp.float32)
    energies = kinetic(slot_map, owner * stick_count, stick_count, length, side)
    partial_corr = lax.dot_general(
        every, projectors, (((1,), (1,)), ((), ())), preferred_element_type=jnp.float32
    ).T
    partial_kin = lax.dot_general(
        energies[None, :] * wide,
        every.astype(jnp.float32),
        (((1,), (1,)), ((), ())),
        precision=highest,
        preferred_element_type=jnp.float32,
    )
    nproj = partial_corr.shape[0]
    packed = jnp.concatenate([partial_corr.reshape(-1), partial_kin.reshape(-1)])
    width = -(-packed.shape[0] // npw)
    packed = jnp.pad(packed, (0, width * npw - packed.shape[0])).reshape(npw, width)
    columns = columns.reshape(npw, total, stick_count)
    columns_hi = lax.reduce_precision(columns, exponent_bits=8, mantissa_bits=7)
    columns_lo = lax.dynamic_slice_in_dim(columns - columns_hi, group * bands, bands, axis=1)
    packed_hi, packed_lo = split2(packed)
    sent = jnp.concatenate(
        [
            columns_hi.reshape(npw, -1).astype(jnp.bfloat16),
            columns_lo.reshape(npw, -1).astype(jnp.bfloat16),
            packed_hi,
            packed_lo,
        ],
        axis=1,
    )
    got = lax.all_to_all(sent, PW, 0, 0, tiled=True)
    nall = total * stick_count
    nown = bands * stick_count
    piece = got[:, :nall].astype(jnp.float32).reshape(npw, total, stick_count)
    mine = lax.dynamic_slice_in_dim(piece, group * bands, bands, axis=1) + got[
        :, nall : nall + nown
    ].astype(jnp.float32).reshape(npw, bands, stick_count)
    owned = jnp.sum(
        got[:, nall + nown : nall + nown + width].astype(jnp.float32)
        + got[:, nall + nown + width :].astype(jnp.float32),
        axis=0,
    )
    grid = jnp.transpose(mine, (1, 0, 2)).reshape(bands, planes, side, side)
    half = jnp.einsum("bzjk,jx->bzxk", grid, side_table, precision=highest)
    real_space = jnp.einsum("bzxk,ky->bzxy", half, side_table, precision=highest)
    weighted = real_space * potential[None]
    back_half = jnp.einsum("bzxy,ky->bzxk", weighted, side_table, precision=highest)
    back_grid = jnp.einsum("bzxk,jx->bzjk", back_half, side_table, precision=highest)
    back_own = back_grid.reshape(bands, side * side)
    piece = lax.dynamic_update_slice_in_dim(piece, mine, group * bands, axis=1)
    plane_gram = lax.dot_general(
        back_own,
        jnp.transpose(piece, (1, 0, 2)).reshape(total, side * side),
        (((1,), (1,)), ((), ())),
        precision=highest,
        preferred_element_type=jnp.float32,
    )
    back = jnp.transpose(back_own.reshape(bands, npw, stick_count), (1, 0, 2))
    ret_sent = jnp.concatenate(
        [
            back.reshape(npw, bands * stick_count),
            jnp.broadcast_to(plane_gram.reshape(1, -1), (npw, bands * total)),
            jnp.broadcast_to(owned[None, :], (npw, width)),
        ],
        axis=1,
    )
    ret = lax.all_to_all(ret_sent, PW, 0, 0, tiled=True)
    returned = ret[:, : bands * stick_count].reshape(npw * planes, bands, stick_count)
    gram_local = jnp.sum(
        ret[:, bands * stick_count : bands * stick_count + bands * total], axis=0
    ).reshape(bands, total)
    reduced = ret[:, bands * stick_count + bands * total :].reshape(-1)
    correlations = reduced[: nproj * total].reshape(nproj, total) / math.sqrt(NG)
    gram_kin = reduced[nproj * total : nproj * total + bands * total].reshape(bands, total)
    spectral = jnp.einsum("zbs,kz->bsk", returned, z_table, precision=highest)
    picked = exact_select(
        spectral.reshape(bands * stick_count, length), on_plane.astype(jnp.bfloat16)
    ).reshape(bands, stick_count, -1)
    local_term = jnp.sum(jnp.where(on_stick.T[None], picked, 0.0), axis=1)
    atoms = species.shape[0]
    per_atom = coupling.shape[1]
    kinds = coupling.shape[0]
    symmetric = 0.5 * (coupling + jnp.swapaxes(coupling, 1, 2))
    onehot = (species[:, None] == jnp.arange(kinds)[None, :]).astype(jnp.float32)
    chosen = jnp.einsum("as,smn->amn", onehot, symmetric, precision=highest)
    weights = jnp.einsum(
        "amn,anb->amb", chosen, correlations.reshape(atoms, per_atom, total), precision=highest
    )
    weights = weights.reshape(atoms * per_atom, total).astype(jnp.bfloat16)
    nonlocal_term = lax.dot_general(
        lax.dynamic_slice_in_dim(weights, group * bands, bands, axis=1), projectors, (((0,), (0,)), ((), ())), preferred_element_type=jnp.float32
    ) / math.sqrt(atoms * per_atom)
    applied = energies[None, :] * wide + local_term + nonlocal_term
    cross = lax.dot_general(
        lax.dynamic_slice_in_dim(correlations, group * bands, bands, axis=1),
        weights.astype(jnp.float32),
        (((0,), (0,)), ((), ())),
        precision=highest,
        preferred_element_type=jnp.float32,
    ) / (math.sqrt(atoms * per_atom) * math.sqrt(NG))
    subspace = (gram_kin + gram_local) / float(NG) + cross
    return (applied, subspace)


def solution(mesh):
    split = Mesh(
        mesh.devices.reshape(mesh.shape["band"], 2, 4, 8, 2),
        ("band", "pw_0", "pw_1", "pw_2", "pw_3"),
    )
    return jax.shard_map(
        local,
        mesh=split,
        in_specs=(P("band", PW), P(PW), P(PW, None, None), P(None, PW), P(), P()),
        out_specs=(P("band", PW), P("band", None)),
        check_vma=False,
    )
```

```python
import math

import jax
import jax.numpy as jnp
from jax import lax
from jax.sharding import Mesh
from jax.sharding import PartitionSpec as P

NSIDE = 96
NG = 884736
PW = ("pw_0", "pw_1", "pw_2", "pw_3")


def one_axis_at_a_time(x, axes):
    for a in axes:
        x = lax.psum(x, a)
    return x


def butterfly(x, axes):
    for a in axes:
        n = lax.axis_size(a)
        d = 1
        while d < n:
            x = x + lax.ppermute(x, a, [(i, i ^ d) for i in range(n)])
            d *= 2
    return x


def cas_table(frequency, length):
    columns = jnp.arange(length)
    phases = frequency[:, None] * columns[None, :] % length
    angles = phases.astype(jnp.float32) * (2.0 * math.pi / length)
    return (jnp.cos(angles) + jnp.sin(angles)) / math.sqrt(length)


def side_frequency(indices):
    halves = (indices + 1) // 2
    return jnp.where(indices % 2 == 1, halves, -halves)


def kinetic(slot_map, first_stick, stick_count, length, side):
    sticks = first_stick + slot_map % stick_count
    plane_index = slot_map // stick_count
    along_z = jnp.where(plane_index < length // 2, plane_index, plane_index - length)
    along_x = side_frequency(sticks // side)
    along_y = side_frequency(sticks % side)
    squared = along_x * along_x + along_y * along_y + along_z * along_z
    return squared.astype(jnp.float32) * (1.0 / (0.5 * side * side + 0.25 * length * length))


def gathered_bands(states, axis):
    n = lax.axis_size(axis)
    copies = jnp.broadcast_to(states[None], (n,) + states.shape)
    every = lax.all_to_all(copies, axis, 0, 0, tiled=True)
    return every.reshape(n * states.shape[0], states.shape[1])


def split3(x):
    hi = lax.reduce_precision(x, exponent_bits=8, mantissa_bits=7)
    rest = x - hi
    mid = lax.reduce_precision(rest, exponent_bits=8, mantissa_bits=7)
    lo = rest - mid
    return hi.astype(jnp.bfloat16), mid.astype(jnp.bfloat16), lo.astype(jnp.bfloat16)


def split2(x):
    hi = lax.reduce_precision(x, exponent_bits=8, mantissa_bits=7)
    return hi.astype(jnp.bfloat16), (x - hi).astype(jnp.bfloat16)


def exact_select(x, onehot):
    hi, lo = split2(x)
    dot = lambda a: jnp.dot(a, onehot, preferred_element_type=jnp.float32)
    return dot(hi) + dot(lo)


def local(states, slot_map, potential, projectors, species, coupling):
    highest = lax.Precision.HIGHEST
    bands = states.shape[0]
    planes = potential.shape[0]
    length = potential.shape[1]
    side = NSIDE
    npw = lax.axis_size(PW)
    stick_count = side * side // npw
    owner = lax.axis_index(PW)
    group = lax.axis_index("band")
    ngroup = lax.axis_size("band")
    every = gathered_bands(states, "band")
    total = every.shape[0]
    count = states.shape[1]
    wide = states.astype(jnp.float32)
    plane_of = slot_map // stick_count
    stick_of = slot_map % stick_count
    on_stick = stick_of[:, None] == jnp.arange(stick_count)[None, :]
    on_plane = jnp.arange(length)[:, None] == plane_of[None, :]
    spread = jnp.where(on_stick[:, None, :], every.T[:, :, None], jnp.zeros((), every.dtype))
    dense = jnp.dot(
        on_plane.astype(jnp.bfloat16),
        spread.reshape(count, total * stick_count),
        preferred_element_type=jnp.float32,
    )
    z_table = cas_table(jnp.arange(length), length)
    side_table = cas_table(side_frequency(jnp.arange(side)), length)
    columns = jnp.dot(z_table.T, dense, precision=lax.Precision.HIGH, preferred_element_type=jnp.float32)
    energies = kinetic(slot_map, owner * stick_count, stick_count, length, side)
    partial_corr = lax.dot_general(
        every, projectors, (((1,), (1,)), ((), ())), preferred_element_type=jnp.float32
    ).T
    partial_kin = lax.dot_general(
        energies[None, :] * wide,
        every.astype(jnp.float32),
        (((1,), (1,)), ((), ())),
        precision=highest,
        preferred_element_type=jnp.float32,
    )
    nproj = partial_corr.shape[0]
    packed = jnp.concatenate([partial_corr.reshape(-1), partial_kin.reshape(-1)])
    width = -(-packed.shape[0] // npw)
    packed = jnp.pad(packed, (0, width * npw - packed.shape[0])).reshape(npw, width)
    columns = columns.reshape(npw, total, stick_count)
    columns_hi = lax.reduce_precision(columns, exponent_bits=8, mantissa_bits=7)
    columns_lo = lax.dynamic_slice_in_dim(columns - columns_hi, group * bands, bands, axis=1)
    packed_hi, packed_lo = split2(packed)
    sent = jnp.concatenate(
        [
            columns_hi.reshape(npw, -1).astype(jnp.bfloat16),
            columns_lo.reshape(npw, -1).astype(jnp.bfloat16),
            packed_hi,
            packed_lo,
        ],
        axis=1,
    )
    got = lax.all_to_all(sent, PW, 0, 0, tiled=True)
    nall = total * stick_count
    nown = bands * stick_count
    piece = got[:, :nall].astype(jnp.float32).reshape(npw, total, stick_count)
    mine = lax.dynamic_slice_in_dim(piece, group * bands, bands, axis=1) + got[
        :, nall : nall + nown
    ].astype(jnp.float32).reshape(npw, bands, stick_count)
    owned = jnp.sum(
        got[:, nall + nown : nall + nown + width].astype(jnp.float32)
        + got[:, nall + nown + width :].astype(jnp.float32),
        axis=0,
    )
    grid = jnp.transpose(mine, (1, 0, 2)).reshape(bands, planes, side, side)
    half = jnp.einsum("bzjk,jx->bzxk", grid, side_table, precision=lax.Precision.HIGH)
    real_space = jnp.einsum("bzxk,ky->bzxy", half, side_table, precision=lax.Precision.HIGH)
    weighted = real_space * potential[None]
    back_half = jnp.einsum("bzxy,ky->bzxk", weighted, side_table, precision=lax.Precision.HIGH)
    back_grid = jnp.einsum("bzxk,jx->bzjk", back_half, side_table, precision=lax.Precision.HIGH)
    back_own = back_grid.reshape(bands, side * side)
    piece = lax.dynamic_update_slice_in_dim(piece, mine, group * bands, axis=1)
    plane_gram = lax.dot_general(
        back_own,
        jnp.transpose(piece, (1, 0, 2)).reshape(total, side * side),
        (((1,), (1,)), ((), ())),
        precision=highest,
        preferred_element_type=jnp.float32,
    )
    back = jnp.transpose(back_own.reshape(bands, npw, stick_count), (1, 0, 2))
    ret_sent = jnp.concatenate(
        [
            back.reshape(npw, bands * stick_count),
            jnp.broadcast_to(plane_gram.reshape(1, -1), (npw, bands * total)),
            jnp.broadcast_to(owned[None, :], (npw, width)),
        ],
        axis=1,
    )
    ret = lax.all_to_all(ret_sent, PW, 0, 0, tiled=True)
    returned = ret[:, : bands * stick_count].reshape(npw * planes, bands, stick_count)
    gram_local = jnp.sum(
        ret[:, bands * stick_count : bands * stick_count + bands * total], axis=0
    ).reshape(bands, total)
    reduced = ret[:, bands * stick_count + bands * total :].reshape(-1)
    correlations = reduced[: nproj * total].reshape(nproj, total) / math.sqrt(NG)
    gram_kin = reduced[nproj * total : nproj * total + bands * total].reshape(bands, total)
    spectral = jnp.einsum("zbs,kz->bsk", returned, z_table, precision=lax.Precision.HIGH)
    picked = exact_select(
        spectral.reshape(bands * stick_count, length), on_plane.astype(jnp.bfloat16)
    ).reshape(bands, stick_count, -1)
    local_term = jnp.sum(jnp.where(on_stick.T[None], picked, 0.0), axis=1)
    atoms = species.shape[0]
    per_atom = coupling.shape[1]
    kinds = coupling.shape[0]
    symmetric = 0.5 * (coupling + jnp.swapaxes(coupling, 1, 2))
    onehot = (species[:, None] == jnp.arange(kinds)[None, :]).astype(jnp.float32)
    chosen = jnp.einsum("as,smn->amn", onehot, symmetric, precision=highest)
    weights = jnp.einsum(
        "amn,anb->amb", chosen, correlations.reshape(atoms, per_atom, total), precision=highest
    )
    weights = weights.reshape(atoms * per_atom, total).astype(jnp.bfloat16)
    nonlocal_term = lax.dot_general(
        lax.dynamic_slice_in_dim(weights, group * bands, bands, axis=1), projectors, (((0,), (0,)), ((), ())), preferred_element_type=jnp.float32
    ) / math.sqrt(atoms * per_atom)
    applied = energies[None, :] * wide + local_term + nonlocal_term
    cross = lax.dot_general(
        lax.dynamic_slice_in_dim(correlations, group * bands, bands, axis=1),
        weights.astype(jnp.float32),
        (((0,), (0,)), ((), ())),
        precision=highest,
        preferred_element_type=jnp.float32,
    ) / (math.sqrt(atoms * per_atom) * math.sqrt(NG))
    subspace = (gram_kin + gram_local) / float(NG) + cross
    return (applied, subspace)


def solution(mesh):
    split = Mesh(
        mesh.devices.reshape(mesh.shape["band"], 2, 4, 8, 2),
        ("band", "pw_0", "pw_1", "pw_2", "pw_3"),
    )
    return jax.shard_map(
        local,
        mesh=split,
        in_specs=(P("band", PW), P(PW), P(PW, None, None), P(None, PW), P(), P()),
        out_specs=(P("band", PW), P("band", None)),
        check_vma=False,
    )
```

```python
import math

import jax
import jax.numpy as jnp
from jax import lax
from jax.sharding import Mesh
from jax.sharding import PartitionSpec as P

NSIDE = 96
NG = 884736
PW = ("pw_0", "pw_1", "pw_2", "pw_3")


def one_axis_at_a_time(x, axes):
    for a in axes:
        x = lax.psum(x, a)
    return x


def butterfly(x, axes):
    for a in axes:
        n = lax.axis_size(a)
        d = 1
        while d < n:
            x = x + lax.ppermute(x, a, [(i, i ^ d) for i in range(n)])
            d *= 2
    return x


def cas_table(frequency, length):
    columns = jnp.arange(length)
    phases = frequency[:, None] * columns[None, :] % length
    angles = phases.astype(jnp.float32) * (2.0 * math.pi / length)
    return (jnp.cos(angles) + jnp.sin(angles)) / math.sqrt(length)


def side_frequency(indices):
    halves = (indices + 1) // 2
    return jnp.where(indices % 2 == 1, halves, -halves)


def kinetic(slot_map, first_stick, stick_count, length, side):
    sticks = first_stick + slot_map % stick_count
    plane_index = slot_map // stick_count
    along_z = jnp.where(plane_index < length // 2, plane_index, plane_index - length)
    along_x = side_frequency(sticks // side)
    along_y = side_frequency(sticks % side)
    squared = along_x * along_x + along_y * along_y + along_z * along_z
    return squared.astype(jnp.float32) * (1.0 / (0.5 * side * side + 0.25 * length * length))


def gathered_bands(states, axis):
    n = lax.axis_size(axis)
    copies = jnp.broadcast_to(states[None], (n,) + states.shape)
    every = lax.all_to_all(copies, axis, 0, 0, tiled=True)
    return every.reshape(n * states.shape[0], states.shape[1])


def split3(x):
    hi = lax.reduce_precision(x, exponent_bits=8, mantissa_bits=7)
    rest = x - hi
    mid = lax.reduce_precision(rest, exponent_bits=8, mantissa_bits=7)
    lo = rest - mid
    return hi.astype(jnp.bfloat16), mid.astype(jnp.bfloat16), lo.astype(jnp.bfloat16)


def split2(x):
    hi = lax.reduce_precision(x, exponent_bits=8, mantissa_bits=7)
    return hi.astype(jnp.bfloat16), (x - hi).astype(jnp.bfloat16)


def exact_select(x, onehot):
    hi, lo = split2(x)
    dot = lambda a: jnp.dot(a, onehot, preferred_element_type=jnp.float32)
    return dot(hi) + dot(lo)


def local(states, slot_map, potential, projectors, species, coupling):
    highest = lax.Precision.HIGHEST
    bands = states.shape[0]
    planes = potential.shape[0]
    length = potential.shape[1]
    side = NSIDE
    npw = lax.axis_size(PW)
    stick_count = side * side // npw
    owner = lax.axis_index(PW)
    group = lax.axis_index("band")
    ngroup = lax.axis_size("band")
    every = gathered_bands(states, "band")
    total = every.shape[0]
    count = states.shape[1]
    wide = states.astype(jnp.float32)
    plane_of = slot_map // stick_count
    stick_of = slot_map % stick_count
    on_stick = stick_of[:, None] == jnp.arange(stick_count)[None, :]
    on_plane = jnp.arange(length)[:, None] == plane_of[None, :]
    spread = jnp.where(on_stick[:, None, :], every.T[:, :, None], jnp.zeros((), every.dtype))
    dense = jnp.dot(
        on_plane.astype(jnp.bfloat16),
        spread.reshape(count, total * stick_count),
        preferred_element_type=jnp.float32,
    )
    z_table = cas_table(jnp.arange(length), length)
    side_table = cas_table(side_frequency(jnp.arange(side)), length)
    columns = jnp.dot(z_table.T, dense, precision=lax.Precision.HIGH, preferred_element_type=jnp.float32)
    energies = kinetic(slot_map, owner * stick_count, stick_count, length, side)
    partial_corr = lax.dot_general(
        every, projectors, (((1,), (1,)), ((), ())), preferred_element_type=jnp.float32
    ).T
    partial_kin = lax.dot_general(
        energies[None, :] * wide,
        every.astype(jnp.float32),
        (((1,), (1,)), ((), ())),
        precision=lax.Precision.HIGH,
        preferred_element_type=jnp.float32,
    )
    nproj = partial_corr.shape[0]
    packed = jnp.concatenate([partial_corr.reshape(-1), partial_kin.reshape(-1)])
    width = -(-packed.shape[0] // npw)
    packed = jnp.pad(packed, (0, width * npw - packed.shape[0])).reshape(npw, width)
    columns = columns.reshape(npw, total, stick_count)
    columns_hi = lax.reduce_precision(columns, exponent_bits=8, mantissa_bits=7)
    columns_lo = lax.dynamic_slice_in_dim(columns - columns_hi, group * bands, bands, axis=1)
    packed_hi, packed_lo = split2(packed)
    sent = jnp.concatenate(
        [
            columns_hi.reshape(npw, -1).astype(jnp.bfloat16),
            columns_lo.reshape(npw, -1).astype(jnp.bfloat16),
            packed_hi,
            packed_lo,
        ],
        axis=1,
    )
    got = lax.all_to_all(sent, PW, 0, 0, tiled=True)
    nall = total * stick_count
    nown = bands * stick_count
    piece = got[:, :nall].astype(jnp.float32).reshape(npw, total, stick_count)
    mine = lax.dynamic_slice_in_dim(piece, group * bands, bands, axis=1) + got[
        :, nall : nall + nown
    ].astype(jnp.float32).reshape(npw, bands, stick_count)
    owned = jnp.sum(
        got[:, nall + nown : nall + nown + width].astype(jnp.float32)
        + got[:, nall + nown + width :].astype(jnp.float32),
        axis=0,
    )
    grid = jnp.transpose(mine, (1, 0, 2)).reshape(bands, planes, side, side)
    half = jnp.einsum("bzjk,jx->bzxk", grid, side_table, precision=lax.Precision.HIGH)
    real_space = jnp.einsum("bzxk,ky->bzxy", half, side_table, precision=lax.Precision.HIGH)
    weighted = real_space * potential[None]
    back_half = jnp.einsum("bzxy,ky->bzxk", weighted, side_table, precision=lax.Precision.HIGH)
    back_grid = jnp.einsum("bzxk,jx->bzjk", back_half, side_table, precision=lax.Precision.HIGH)
    back_own = back_grid.reshape(bands, side * side)
    piece = lax.dynamic_update_slice_in_dim(piece, mine, group * bands, axis=1)
    plane_gram = lax.dot_general(
        back_own,
        jnp.transpose(piece, (1, 0, 2)).reshape(total, side * side),
        (((1,), (1,)), ((), ())),
        precision=lax.Precision.HIGH,
        preferred_element_type=jnp.float32,
    )
    back = jnp.transpose(back_own.reshape(bands, npw, stick_count), (1, 0, 2))
    ret_sent = jnp.concatenate(
        [
            back.reshape(npw, bands * stick_count),
            jnp.broadcast_to(plane_gram.reshape(1, -1), (npw, bands * total)),
            jnp.broadcast_to(owned[None, :], (npw, width)),
        ],
        axis=1,
    )
    ret = lax.all_to_all(ret_sent, PW, 0, 0, tiled=True)
    returned = ret[:, : bands * stick_count].reshape(npw * planes, bands, stick_count)
    gram_local = jnp.sum(
        ret[:, bands * stick_count : bands * stick_count + bands * total], axis=0
    ).reshape(bands, total)
    reduced = ret[:, bands * stick_count + bands * total :].reshape(-1)
    correlations = reduced[: nproj * total].reshape(nproj, total) / math.sqrt(NG)
    gram_kin = reduced[nproj * total : nproj * total + bands * total].reshape(bands, total)
    spectral = jnp.einsum("zbs,kz->bsk", returned, z_table, precision=lax.Precision.HIGH)
    picked = exact_select(
        spectral.reshape(bands * stick_count, length), on_plane.astype(jnp.bfloat16)
    ).reshape(bands, stick_count, -1)
    local_term = jnp.sum(jnp.where(on_stick.T[None], picked, 0.0), axis=1)
    atoms = species.shape[0]
    per_atom = coupling.shape[1]
    kinds = coupling.shape[0]
    symmetric = 0.5 * (coupling + jnp.swapaxes(coupling, 1, 2))
    onehot = (species[:, None] == jnp.arange(kinds)[None, :]).astype(jnp.float32)
    chosen = jnp.einsum("as,smn->amn", onehot, symmetric, precision=highest)
    weights = jnp.einsum(
        "amn,anb->amb", chosen, correlations.reshape(atoms, per_atom, total), precision=highest
    )
    weights = weights.reshape(atoms * per_atom, total).astype(jnp.bfloat16)
    nonlocal_term = lax.dot_general(
        lax.dynamic_slice_in_dim(weights, group * bands, bands, axis=1), projectors, (((0,), (0,)), ((), ())), preferred_element_type=jnp.float32
    ) / math.sqrt(atoms * per_atom)
    applied = energies[None, :] * wide + local_term + nonlocal_term
    cross = lax.dot_general(
        lax.dynamic_slice_in_dim(correlations, group * bands, bands, axis=1),
        weights.astype(jnp.float32),
        (((0,), (0,)), ((), ())),
        precision=highest,
        preferred_element_type=jnp.float32,
    ) / (math.sqrt(atoms * per_atom) * math.sqrt(NG))
    subspace = (gram_kin + gram_local) / float(NG) + cross
    return (applied, subspace)


def solution(mesh):
    split = Mesh(
        mesh.devices.reshape(mesh.shape["band"], 2, 4, 8, 2),
        ("band", "pw_0", "pw_1", "pw_2", "pw_3"),
    )
    return jax.shard_map(
        local,
        mesh=split,
        in_specs=(P("band", PW), P(PW), P(PW, None, None), P(None, PW), P(), P()),
        out_specs=(P("band", PW), P("band", None)),
        check_vma=False,
    )
```

```python
import math

import jax
import jax.numpy as jnp
from jax import lax
from jax.sharding import Mesh
from jax.sharding import PartitionSpec as P

NSIDE = 96
NG = 884736
PW = ("pw_0", "pw_1", "pw_2", "pw_3")


def one_axis_at_a_time(x, axes):
    for a in axes:
        x = lax.psum(x, a)
    return x


def butterfly(x, axes):
    for a in axes:
        n = lax.axis_size(a)
        d = 1
        while d < n:
            x = x + lax.ppermute(x, a, [(i, i ^ d) for i in range(n)])
            d *= 2
    return x


def cas_table(frequency, length):
    columns = jnp.arange(length)
    phases = frequency[:, None] * columns[None, :] % length
    angles = phases.astype(jnp.float32) * (2.0 * math.pi / length)
    return (jnp.cos(angles) + jnp.sin(angles)) / math.sqrt(length)


def side_frequency(indices):
    halves = (indices + 1) // 2
    return jnp.where(indices % 2 == 1, halves, -halves)


def kinetic(slot_map, first_stick, stick_count, length, side):
    sticks = first_stick + slot_map % stick_count
    plane_index = slot_map // stick_count
    along_z = jnp.where(plane_index < length // 2, plane_index, plane_index - length)
    along_x = side_frequency(sticks // side)
    along_y = side_frequency(sticks % side)
    squared = along_x * along_x + along_y * along_y + along_z * along_z
    return squared.astype(jnp.float32) * (1.0 / (0.5 * side * side + 0.25 * length * length))


def gathered_bands(states, axis):
    n = lax.axis_size(axis)
    copies = jnp.broadcast_to(states[None], (n,) + states.shape)
    every = lax.all_to_all(copies, axis, 0, 0, tiled=True)
    return every.reshape(n * states.shape[0], states.shape[1])


def split3(x):
    hi = lax.reduce_precision(x, exponent_bits=8, mantissa_bits=7)
    rest = x - hi
    mid = lax.reduce_precision(rest, exponent_bits=8, mantissa_bits=7)
    lo = rest - mid
    return hi.astype(jnp.bfloat16), mid.astype(jnp.bfloat16), lo.astype(jnp.bfloat16)


def split2(x):
    hi = lax.reduce_precision(x, exponent_bits=8, mantissa_bits=7)
    return hi.astype(jnp.bfloat16), (x - hi).astype(jnp.bfloat16)


def exact_select(x, onehot):
    hi, lo = split2(x)
    dot = lambda a: jnp.dot(a, onehot, preferred_element_type=jnp.float32)
    return dot(hi) + dot(lo)


def local(states, slot_map, potential, projectors, species, coupling):
    highest = lax.Precision.HIGHEST
    bands = states.shape[0]
    planes = potential.shape[0]
    length = potential.shape[1]
    side = NSIDE
    npw = lax.axis_size(PW)
    stick_count = side * side // npw
    owner = lax.axis_index(PW)
    group = lax.axis_index("band")
    ngroup = lax.axis_size("band")
    every = gathered_bands(states, "band")
    total = every.shape[0]
    count = states.shape[1]
    wide = states.astype(jnp.float32)
    plane_of = slot_map // stick_count
    stick_of = slot_map % stick_count
    on_stick = stick_of[:, None] == jnp.arange(stick_count)[None, :]
    on_plane = jnp.arange(length)[:, None] == plane_of[None, :]
    z_table = cas_table(jnp.arange(length), length)
    side_table = cas_table(side_frequency(jnp.arange(side)), length)
    plane_bf16 = on_plane.astype(jnp.bfloat16)

    def z_columns(rows):
        spread = jnp.where(on_stick[:, None, :], rows.T[:, :, None], jnp.zeros((), rows.dtype))
        dense = jnp.dot(
            plane_bf16, spread.reshape(count, -1), preferred_element_type=jnp.float32
        )
        cols = jnp.dot(z_table.T, dense, precision=lax.Precision.HIGH, preferred_element_type=jnp.float32)
        return cols.reshape(npw, rows.shape[0] * stick_count)

    own_columns = z_columns(states)
    doubled = jnp.concatenate([every, every], axis=0)
    others = lax.dynamic_slice_in_dim(doubled, (group + 1) * bands, total - bands, axis=0)
    other_columns = z_columns(others)
    energies = kinetic(slot_map, owner * stick_count, stick_count, length, side)
    partial_corr = lax.dot_general(
        every, projectors, (((1,), (1,)), ((), ())), preferred_element_type=jnp.float32
    ).T
    partial_kin = lax.dot_general(
        energies[None, :] * wide,
        every.astype(jnp.float32),
        (((1,), (1,)), ((), ())),
        precision=lax.Precision.HIGH,
        preferred_element_type=jnp.float32,
    )
    nproj = partial_corr.shape[0]
    packed = jnp.concatenate([partial_corr.reshape(-1), partial_kin.reshape(-1)])
    width = -(-packed.shape[0] // npw)
    packed = jnp.pad(packed, (0, width * npw - packed.shape[0])).reshape(npw, width)
    own_hi, own_lo = split2(own_columns)
    packed_hi, packed_lo = split2(packed)
    sent = jnp.concatenate(
        [own_hi, own_lo, other_columns.astype(jnp.bfloat16), packed_hi, packed_lo], axis=1
    )
    got = lax.all_to_all(sent, PW, 0, 0, tiled=True)
    nown = bands * stick_count
    noth = (total - bands) * stick_count
    mine = (
        got[:, :nown].astype(jnp.float32) + got[:, nown : 2 * nown].astype(jnp.float32)
    ).reshape(npw, bands, stick_count)
    rest = got[:, 2 * nown : 2 * nown + noth].astype(jnp.float32).reshape(npw, total - bands, stick_count)
    tail = 2 * nown + noth
    owned = jnp.sum(
        got[:, tail : tail + width].astype(jnp.float32)
        + got[:, tail + width : tail + 2 * width].astype(jnp.float32),
        axis=0,
    )
    piece = jnp.concatenate([mine, rest], axis=1)
    grid = jnp.transpose(mine, (1, 0, 2)).reshape(bands, planes, side, side)
    half = jnp.einsum("bzjk,jx->bzxk", grid, side_table, precision=lax.Precision.HIGH)
    real_space = jnp.einsum("bzxk,ky->bzxy", half, side_table, precision=lax.Precision.HIGH)
    weighted = real_space * potential[None]
    back_half = jnp.einsum("bzxy,ky->bzxk", weighted, side_table, precision=lax.Precision.HIGH)
    back_grid = jnp.einsum("bzxk,jx->bzjk", back_half, side_table, precision=lax.Precision.HIGH)
    back_own = back_grid.reshape(bands, side * side)
    plane_gram = lax.dot_general(
        back_own,
        jnp.transpose(piece, (1, 0, 2)).reshape(total, side * side),
        (((1,), (1,)), ((), ())),
        precision=lax.Precision.HIGH,
        preferred_element_type=jnp.float32,
    )
    back = jnp.transpose(back_own.reshape(bands, npw, stick_count), (1, 0, 2))
    ret_sent = jnp.concatenate(
        [
            back.reshape(npw, bands * stick_count),
            jnp.broadcast_to(plane_gram.reshape(1, -1), (npw, bands * total)),
            jnp.broadcast_to(owned[None, :], (npw, width)),
        ],
        axis=1,
    )
    ret = lax.all_to_all(ret_sent, PW, 0, 0, tiled=True)
    returned = ret[:, : bands * stick_count].reshape(npw * planes, bands, stick_count)
    gram_local = jnp.sum(
        ret[:, bands * stick_count : bands * stick_count + bands * total], axis=0
    ).reshape(bands, ngroup, bands)
    gram_local = jnp.take(gram_local, (jnp.arange(ngroup) - group) % ngroup, axis=1).reshape(bands, total)
    reduced = ret[:, bands * stick_count + bands * total :].reshape(-1)
    correlations = reduced[: nproj * total].reshape(nproj, total) / math.sqrt(NG)
    gram_kin = reduced[nproj * total : nproj * total + bands * total].reshape(bands, total)
    spectral = jnp.einsum("zbs,kz->bsk", returned, z_table, precision=lax.Precision.HIGH)
    picked = exact_select(
        spectral.reshape(bands * stick_count, length), on_plane.astype(jnp.bfloat16)
    ).reshape(bands, stick_count, -1)
    local_term = jnp.sum(jnp.where(on_stick.T[None], picked, 0.0), axis=1)
    atoms = species.shape[0]
    per_atom = coupling.shape[1]
    kinds = coupling.shape[0]
    symmetric = 0.5 * (coupling + jnp.swapaxes(coupling, 1, 2))
    onehot = (species[:, None] == jnp.arange(kinds)[None, :]).astype(jnp.float32)
    chosen = jnp.einsum("as,smn->amn", onehot, symmetric, precision=highest)
    weights = jnp.einsum(
        "amn,anb->amb", chosen, correlations.reshape(atoms, per_atom, total), precision=highest
    )
    weights = weights.reshape(atoms * per_atom, total).astype(jnp.bfloat16)
    nonlocal_term = lax.dot_general(
        lax.dynamic_slice_in_dim(weights, group * bands, bands, axis=1), projectors, (((0,), (0,)), ((), ())), preferred_element_type=jnp.float32
    ) / math.sqrt(atoms * per_atom)
    applied = energies[None, :] * wide + local_term + nonlocal_term
    cross = lax.dot_general(
        lax.dynamic_slice_in_dim(correlations, group * bands, bands, axis=1),
        weights.astype(jnp.float32),
        (((0,), (0,)), ((), ())),
        precision=highest,
        preferred_element_type=jnp.float32,
    ) / (math.sqrt(atoms * per_atom) * math.sqrt(NG))
    subspace = (gram_kin + gram_local) / float(NG) + cross
    return (applied, subspace)


def solution(mesh):
    split = Mesh(
        mesh.devices.reshape(mesh.shape["band"], 2, 4, 8, 2),
        ("band", "pw_0", "pw_1", "pw_2", "pw_3"),
    )
    return jax.shard_map(
        local,
        mesh=split,
        in_specs=(P("band", PW), P(PW), P(PW, None, None), P(None, PW), P(), P()),
        out_specs=(P("band", PW), P("band", None)),
        check_vma=False,
    )
```

```python
import math

import jax
import jax.numpy as jnp
from jax import lax
from jax.sharding import Mesh
from jax.sharding import PartitionSpec as P

NSIDE = 96
NG = 884736
PW = ("pw_0", "pw_1", "pw_2", "pw_3")


def one_axis_at_a_time(x, axes):
    for a in axes:
        x = lax.psum(x, a)
    return x


def butterfly(x, axes):
    for a in axes:
        n = lax.axis_size(a)
        d = 1
        while d < n:
            x = x + lax.ppermute(x, a, [(i, i ^ d) for i in range(n)])
            d *= 2
    return x


def cas_table(frequency, length):
    columns = jnp.arange(length)
    phases = frequency[:, None] * columns[None, :] % length
    angles = phases.astype(jnp.float32) * (2.0 * math.pi / length)
    return (jnp.cos(angles) + jnp.sin(angles)) / math.sqrt(length)


def side_frequency(indices):
    halves = (indices + 1) // 2
    return jnp.where(indices % 2 == 1, halves, -halves)


def kinetic(slot_map, first_stick, stick_count, length, side):
    sticks = first_stick + slot_map % stick_count
    plane_index = slot_map // stick_count
    along_z = jnp.where(plane_index < length // 2, plane_index, plane_index - length)
    along_x = side_frequency(sticks // side)
    along_y = side_frequency(sticks % side)
    squared = along_x * along_x + along_y * along_y + along_z * along_z
    return squared.astype(jnp.float32) * (1.0 / (0.5 * side * side + 0.25 * length * length))


def gathered_bands(states, axis):
    n = lax.axis_size(axis)
    copies = jnp.broadcast_to(states[None], (n,) + states.shape)
    every = lax.all_to_all(copies, axis, 0, 0, tiled=True)
    return every.reshape(n * states.shape[0], states.shape[1])


def split3(x):
    hi = lax.reduce_precision(x, exponent_bits=8, mantissa_bits=7)
    rest = x - hi
    mid = lax.reduce_precision(rest, exponent_bits=8, mantissa_bits=7)
    lo = rest - mid
    return hi.astype(jnp.bfloat16), mid.astype(jnp.bfloat16), lo.astype(jnp.bfloat16)


def split2(x):
    hi = lax.reduce_precision(x, exponent_bits=8, mantissa_bits=7)
    return hi.astype(jnp.bfloat16), (x - hi).astype(jnp.bfloat16)


def exact_select(x, onehot):
    hi, lo = split2(x)
    both = jnp.dot(jnp.concatenate([hi, lo], axis=0), onehot, preferred_element_type=jnp.float32)
    return both[: x.shape[0]] + both[x.shape[0] :]


def local(states, slot_map, potential, projectors, species, coupling):
    highest = lax.Precision.HIGHEST
    bands = states.shape[0]
    planes = potential.shape[0]
    length = potential.shape[1]
    side = NSIDE
    npw = lax.axis_size(PW)
    stick_count = side * side // npw
    owner = lax.axis_index(PW)
    group = lax.axis_index("band")
    ngroup = lax.axis_size("band")
    every = gathered_bands(states, "band")
    total = every.shape[0]
    count = states.shape[1]
    wide = states.astype(jnp.float32)
    plane_of = slot_map // stick_count
    stick_of = slot_map % stick_count
    on_stick = stick_of[:, None] == jnp.arange(stick_count)[None, :]
    on_plane = jnp.arange(length)[:, None] == plane_of[None, :]
    spread = jnp.where(on_stick[:, None, :], every.T[:, :, None], jnp.zeros((), every.dtype))
    dense = jnp.dot(
        on_plane.astype(jnp.bfloat16),
        spread.reshape(count, total * stick_count),
        preferred_element_type=jnp.float32,
    )
    z_table = cas_table(jnp.arange(length), length)
    side_table = cas_table(side_frequency(jnp.arange(side)), length)
    columns = jnp.dot(z_table.T, dense, precision=lax.Precision.HIGH, preferred_element_type=jnp.float32)
    energies = kinetic(slot_map, owner * stick_count, stick_count, length, side)
    partial_corr = lax.dot_general(
        every, projectors, (((1,), (1,)), ((), ())), preferred_element_type=jnp.float32
    ).T
    partial_kin = lax.dot_general(
        energies[None, :] * wide,
        every.astype(jnp.float32),
        (((1,), (1,)), ((), ())),
        precision=lax.Precision.HIGH,
        preferred_element_type=jnp.float32,
    )
    nproj = partial_corr.shape[0]
    packed = jnp.concatenate([partial_corr.reshape(-1), partial_kin.reshape(-1)])
    width = -(-packed.shape[0] // npw)
    packed = jnp.pad(packed, (0, width * npw - packed.shape[0])).reshape(npw, width)
    columns = columns.reshape(npw, total, stick_count)
    columns_hi = lax.reduce_precision(columns, exponent_bits=8, mantissa_bits=7)
    columns_lo = lax.dynamic_slice_in_dim(columns - columns_hi, group * bands, bands, axis=1)
    packed_hi, packed_lo = split2(packed)
    sent = jnp.concatenate(
        [
            columns_hi.reshape(npw, -1).astype(jnp.bfloat16),
            columns_lo.reshape(npw, -1).astype(jnp.bfloat16),
            packed_hi,
            packed_lo,
        ],
        axis=1,
    )
    got = lax.all_to_all(sent, PW, 0, 0, tiled=True)
    nall = total * stick_count
    nown = bands * stick_count
    piece = got[:, :nall].astype(jnp.float32).reshape(npw, total, stick_count)
    mine = lax.dynamic_slice_in_dim(piece, group * bands, bands, axis=1) + got[
        :, nall : nall + nown
    ].astype(jnp.float32).reshape(npw, bands, stick_count)
    owned = jnp.sum(
        got[:, nall + nown : nall + nown + width].astype(jnp.float32)
        + got[:, nall + nown + width :].astype(jnp.float32),
        axis=0,
    )
    grid = jnp.transpose(mine, (1, 0, 2)).reshape(bands, planes, side, side)
    half = jnp.einsum("bzjk,jx->bzxk", grid, side_table, precision=lax.Precision.HIGH)
    real_space = jnp.einsum("bzxk,ky->bzxy", half, side_table, precision=lax.Precision.HIGH)
    weighted = real_space * potential[None]
    back_half = jnp.einsum("bzxy,ky->bzxk", weighted, side_table, precision=lax.Precision.HIGH)
    back_grid = jnp.einsum("bzxk,jx->bzjk", back_half, side_table, precision=lax.Precision.HIGH)
    back_own = back_grid.reshape(bands, side * side)
    piece = lax.dynamic_update_slice_in_dim(piece, mine, group * bands, axis=1)
    plane_gram = lax.dot_general(
        back_own,
        jnp.transpose(piece, (1, 0, 2)).reshape(total, side * side),
        (((1,), (1,)), ((), ())),
        precision=lax.Precision.HIGH,
        preferred_element_type=jnp.float32,
    )
    back = jnp.transpose(back_own.reshape(bands, npw, stick_count), (1, 0, 2))
    ret_sent = jnp.concatenate(
        [
            back.reshape(npw, bands * stick_count),
            jnp.broadcast_to(plane_gram.reshape(1, -1), (npw, bands * total)),
            jnp.broadcast_to(owned[None, :], (npw, width)),
        ],
        axis=1,
    )
    ret = lax.all_to_all(ret_sent, PW, 0, 0, tiled=True)
    returned = ret[:, : bands * stick_count].reshape(npw * planes, bands, stick_count)
    gram_local = jnp.sum(
        ret[:, bands * stick_count : bands * stick_count + bands * total], axis=0
    ).reshape(bands, total)
    reduced = ret[:, bands * stick_count + bands * total :].reshape(-1)
    correlations = reduced[: nproj * total].reshape(nproj, total) / math.sqrt(NG)
    gram_kin = reduced[nproj * total : nproj * total + bands * total].reshape(bands, total)
    spectral = jnp.einsum("zbs,kz->bsk", returned, z_table, precision=lax.Precision.HIGH)
    picked = exact_select(
        spectral.reshape(bands * stick_count, length), on_plane.astype(jnp.bfloat16)
    ).reshape(bands, stick_count, -1)
    local_term = jnp.sum(jnp.where(on_stick.T[None], picked, 0.0), axis=1)
    atoms = species.shape[0]
    per_atom = coupling.shape[1]
    kinds = coupling.shape[0]
    symmetric = 0.5 * (coupling + jnp.swapaxes(coupling, 1, 2))
    onehot = (species[:, None] == jnp.arange(kinds)[None, :]).astype(jnp.float32)
    chosen = jnp.einsum("as,smn->amn", onehot, symmetric, precision=highest)
    weights = jnp.einsum(
        "amn,anb->amb", chosen, correlations.reshape(atoms, per_atom, total), precision=highest
    )
    weights = weights.reshape(atoms * per_atom, total).astype(jnp.bfloat16)
    nonlocal_term = lax.dot_general(
        lax.dynamic_slice_in_dim(weights, group * bands, bands, axis=1), projectors, (((0,), (0,)), ((), ())), preferred_element_type=jnp.float32
    ) / math.sqrt(atoms * per_atom)
    applied = energies[None, :] * wide + local_term + nonlocal_term
    cross = lax.dot_general(
        lax.dynamic_slice_in_dim(correlations, group * bands, bands, axis=1),
        weights.astype(jnp.float32),
        (((0,), (0,)), ((), ())),
        precision=highest,
        preferred_element_type=jnp.float32,
    ) / (math.sqrt(atoms * per_atom) * math.sqrt(NG))
    subspace = (gram_kin + gram_local) / float(NG) + cross
    return (applied, subspace)


def solution(mesh):
    split = Mesh(
        mesh.devices.reshape(mesh.shape["band"], 2, 4, 8, 2),
        ("band", "pw_0", "pw_1", "pw_2", "pw_3"),
    )
    return jax.shard_map(
        local,
        mesh=split,
        in_specs=(P("band", PW), P(PW), P(PW, None, None), P(None, PW), P(), P()),
        out_specs=(P("band", PW), P("band", None)),
        check_vma=False,
    )
```

```python
import math

import jax
import jax.numpy as jnp
from jax import lax
from jax.sharding import Mesh
from jax.sharding import PartitionSpec as P

NSIDE = 96
NG = 884736
PW = ("pw_0", "pw_1", "pw_2", "pw_3")


def one_axis_at_a_time(x, axes):
    for a in axes:
        x = lax.psum(x, a)
    return x


def butterfly(x, axes):
    for a in axes:
        n = lax.axis_size(a)
        d = 1
        while d < n:
            x = x + lax.ppermute(x, a, [(i, i ^ d) for i in range(n)])
            d *= 2
    return x


def cas_table(frequency, length):
    columns = jnp.arange(length)
    phases = frequency[:, None] * columns[None, :] % length
    angles = phases.astype(jnp.float32) * (2.0 * math.pi / length)
    return (jnp.cos(angles) + jnp.sin(angles)) / math.sqrt(length)


def side_frequency(indices):
    halves = (indices + 1) // 2
    return jnp.where(indices % 2 == 1, halves, -halves)


def kinetic(slot_map, first_stick, stick_count, length, side):
    sticks = first_stick + slot_map % stick_count
    plane_index = slot_map // stick_count
    along_z = jnp.where(plane_index < length // 2, plane_index, plane_index - length)
    along_x = side_frequency(sticks // side)
    along_y = side_frequency(sticks % side)
    squared = along_x * along_x + along_y * along_y + along_z * along_z
    return squared.astype(jnp.float32) * (1.0 / (0.5 * side * side + 0.25 * length * length))


def gathered_bands(states, axis):
    n = lax.axis_size(axis)
    copies = jnp.broadcast_to(states[None], (n,) + states.shape)
    every = lax.all_to_all(copies, axis, 0, 0, tiled=True)
    return every.reshape(n * states.shape[0], states.shape[1])


def split3(x):
    hi = lax.reduce_precision(x, exponent_bits=8, mantissa_bits=7)
    rest = x - hi
    mid = lax.reduce_precision(rest, exponent_bits=8, mantissa_bits=7)
    lo = rest - mid
    return hi.astype(jnp.bfloat16), mid.astype(jnp.bfloat16), lo.astype(jnp.bfloat16)


def split2(x):
    hi = lax.reduce_precision(x, exponent_bits=8, mantissa_bits=7)
    return hi.astype(jnp.bfloat16), (x - hi).astype(jnp.bfloat16)


def exact_select(x, onehot):
    hi, lo = split2(x)
    dot = lambda a: jnp.dot(a, onehot, preferred_element_type=jnp.float32)
    return dot(hi) + dot(lo)


def local(states, slot_map, potential, projectors, species, coupling):
    highest = lax.Precision.HIGHEST
    bands = states.shape[0]
    planes = potential.shape[0]
    length = potential.shape[1]
    side = NSIDE
    npw = lax.axis_size(PW)
    stick_count = side * side // npw
    owner = lax.axis_index(PW)
    group = lax.axis_index("band")
    ngroup = lax.axis_size("band")
    every = gathered_bands(states, "band")
    total = every.shape[0]
    count = states.shape[1]
    wide = states.astype(jnp.float32)
    plane_of = slot_map // stick_count
    stick_of = slot_map % stick_count
    on_stick = stick_of[:, None] == jnp.arange(stick_count)[None, :]
    on_plane = jnp.arange(length)[:, None] == plane_of[None, :]
    spread = jnp.where(on_stick[:, None, :], every.T[:, :, None], jnp.zeros((), every.dtype))
    dense = jnp.dot(
        on_plane.astype(jnp.bfloat16),
        spread.reshape(count, total * stick_count),
        preferred_element_type=jnp.float32,
    )
    z_table = cas_table(jnp.arange(length), length)
    side_table = cas_table(side_frequency(jnp.arange(side)), length)
    columns = jnp.dot(z_table.T, dense, precision=lax.Precision.HIGH, preferred_element_type=jnp.float32)
    energies = kinetic(slot_map, owner * stick_count, stick_count, length, side)
    partial_corr = lax.dot_general(
        every, projectors, (((1,), (1,)), ((), ())), preferred_element_type=jnp.float32
    ).T
    partial_kin = lax.dot_general(
        energies[None, :] * wide,
        every.astype(jnp.float32),
        (((1,), (1,)), ((), ())),
        precision=lax.Precision.HIGH,
        preferred_element_type=jnp.float32,
    )
    nproj = partial_corr.shape[0]
    packed = jnp.concatenate([partial_corr.reshape(-1), partial_kin.reshape(-1)])
    width = -(-packed.shape[0] // npw)
    packed = jnp.pad(packed, (0, width * npw - packed.shape[0])).reshape(npw, width)
    columns = columns.reshape(npw, total, stick_count)
    columns_hi = lax.reduce_precision(columns, exponent_bits=8, mantissa_bits=7)
    columns_lo = lax.dynamic_slice_in_dim(columns - columns_hi, group * bands, bands, axis=1)
    packed_hi, packed_lo = split2(packed)
    sent = jnp.concatenate(
        [
            columns_hi.reshape(npw, -1).astype(jnp.bfloat16),
            columns_lo.reshape(npw, -1).astype(jnp.bfloat16),
            packed_hi,
            packed_lo,
        ],
        axis=1,
    )
    got = lax.all_to_all(sent, PW, 0, 0, tiled=True)
    nall = total * stick_count
    nown = bands * stick_count
    piece = got[:, :nall].astype(jnp.float32).reshape(npw, total, stick_count)
    mine = lax.dynamic_slice_in_dim(piece, group * bands, bands, axis=1) + got[
        :, nall : nall + nown
    ].astype(jnp.float32).reshape(npw, bands, stick_count)
    owned = jnp.sum(
        got[:, nall + nown : nall + nown + width].astype(jnp.float32)
        + got[:, nall + nown + width :].astype(jnp.float32),
        axis=0,
    )
    grid = jnp.transpose(mine, (1, 0, 2)).reshape(bands, planes, side, side)
    half = jnp.einsum("bzjk,jx->bzxk", grid, side_table, precision=lax.Precision.HIGH)
    real_space = jnp.einsum("bzxk,ky->bzxy", half, side_table, precision=lax.Precision.HIGH)
    weighted = real_space * potential[None]
    back_half = jnp.einsum("bzxy,ky->bzxk", weighted, side_table, precision=lax.Precision.HIGH)
    back_grid = jnp.einsum("bzxk,jx->bzjk", back_half, side_table, precision=lax.Precision.HIGH)
    back_own = back_grid.reshape(bands, side * side)
    piece = lax.dynamic_update_slice_in_dim(piece, mine, group * bands, axis=1)
    plane_gram = lax.dot_general(
        back_own,
        jnp.transpose(piece, (1, 0, 2)).reshape(total, side * side),
        (((1,), (1,)), ((), ())),
        precision=lax.Precision.HIGH,
        preferred_element_type=jnp.float32,
    )
    back = jnp.transpose(back_own.reshape(bands, npw, stick_count), (1, 0, 2))
    ret_sent = jnp.concatenate(
        [
            back.reshape(npw, bands * stick_count),
            jnp.broadcast_to(plane_gram.reshape(1, -1), (npw, bands * total)),
            jnp.broadcast_to(owned[None, :], (npw, width)),
        ],
        axis=1,
    )
    ret = lax.all_to_all(ret_sent, PW, 0, 0, tiled=True)
    returned = ret[:, : bands * stick_count].reshape(npw * planes, bands, stick_count)
    gram_local = jnp.sum(
        ret[:, bands * stick_count : bands * stick_count + bands * total], axis=0
    ).reshape(bands, total)
    reduced = ret[:, bands * stick_count + bands * total :].reshape(-1)
    correlations = reduced[: nproj * total].reshape(nproj, total) / math.sqrt(NG)
    gram_kin = reduced[nproj * total : nproj * total + bands * total].reshape(bands, total)
    spectral = jnp.einsum("zbs,kz->bsk", returned, z_table, precision=lax.Precision.HIGH)
    picked = exact_select(
        spectral.reshape(bands * stick_count, length), on_plane.astype(jnp.bfloat16)
    ).reshape(bands, stick_count, -1)
    local_term = jnp.sum(jnp.where(on_stick.T[None], picked, 0.0), axis=1)
    atoms = species.shape[0]
    per_atom = coupling.shape[1]
    kinds = coupling.shape[0]
    symmetric = 0.5 * (coupling + jnp.swapaxes(coupling, 1, 2))
    onehot = (species[:, None] == jnp.arange(kinds)[None, :]).astype(jnp.float32)
    chosen = jnp.einsum("as,smn->amn", onehot, symmetric, precision=lax.Precision.HIGH)
    weights = jnp.einsum(
        "amn,anb->amb", chosen, correlations.reshape(atoms, per_atom, total), precision=lax.Precision.HIGH
    )
    weights = weights.reshape(atoms * per_atom, total).astype(jnp.bfloat16)
    nonlocal_term = lax.dot_general(
        lax.dynamic_slice_in_dim(weights, group * bands, bands, axis=1), projectors, (((0,), (0,)), ((), ())), preferred_element_type=jnp.float32
    ) / math.sqrt(atoms * per_atom)
    applied = energies[None, :] * wide + local_term + nonlocal_term
    cross = lax.dot_general(
        lax.dynamic_slice_in_dim(correlations, group * bands, bands, axis=1),
        weights.astype(jnp.float32),
        (((0,), (0,)), ((), ())),
        precision=lax.Precision.HIGH,
        preferred_element_type=jnp.float32,
    ) / (math.sqrt(atoms * per_atom) * math.sqrt(NG))
    subspace = (gram_kin + gram_local) / float(NG) + cross
    return (applied, subspace)


def solution(mesh):
    split = Mesh(
        mesh.devices.reshape(mesh.shape["band"], 2, 4, 8, 2),
        ("band", "pw_0", "pw_1", "pw_2", "pw_3"),
    )
    return jax.shard_map(
        local,
        mesh=split,
        in_specs=(P("band", PW), P(PW), P(PW, None, None), P(None, PW), P(), P()),
        out_specs=(P("band", PW), P("band", None)),
        check_vma=False,
    )
```
